512 devices in a mesh: section: 64 (over y_hi, z, x), rep: 8 (over y_lo, core).
Axes of the slice: x: 4, y: 8 (y_hi: 2, y_lo: 4; y = y_hi * 4 + y_lo), z: 8, core: 2. Of those that a mesh axis runs over, the one named last changes fastest.
Arguments:
- features: bfloat16 [65536, 512], P(('section', 'rep')), may hold values from -6 to 6
- col_panels: int32 [512, 8, 12], P('section', 'rep'), may hold values from 0 to 511, as said below
- block_counts: int32 [512, 8], P('section', 'rep'), may hold values from 1 to 12, as said below
- block_values: bfloat16 [512, 8, 12, 128, 128], P('section', 'rep'), may hold values from 0.0019989014 to 0.019897461
- weight: bfloat16 [512, 512], replicated, may hold values from -0.25 to 0.25
- bias: float32 [512], replicated, may hold values from -3 to 3
- cotangent: bfloat16 [65536, 512], P(('section', 'rep')), may hold values from -6 to 6
Outputs:
- hidden: bfloat16 [65536, 512], P(('section', 'rep'))
- weight_grad: float32 [512, 512], replicated
- bias_grad: float32 [512], replicated
The draws below stay inside these ranges and needn't reach their ends.
Inputs may be any that keep to these rules, and one draw needn't show every extreme that they name: Column group r holds the column panels c with (c) % 8 == r; col_panels[p, r, k] lies in column group r, and the 12 entries of one list are distinct. Only the first block_counts[p, r] slots of a list are nonzero blocks; later slots are ignored. The count 12 occurs in every draw.
All inputs are finite; a program needn't handle non-finite values.
Results may differ from the reference program's by a relative error of at most 0.0055.
Values may be sent and summed in bfloat16 or wider, within the bound.
No kernel may reach another device: no remote copies, remote signals or barrier semaphores. Data moves between devices by JAX's collectives and lax.ppermute only.
A program may use at most 64 MiB of HBM per device.

```python
import math
import jax
import jax.numpy as jnp
from jax import lax

BLOCK = 128
WIDTH = 512
PANELS_DEV = 1
REPS = 8
GROUP = 8
PANELS = 512
NODES = 65536
COLUMNS = 64
SLOTS = 12


def draw_col_panels(key, part):
    scores = jax.random.randint(key, (PANELS, REPS, COLUMNS), 0, 1 << 20) * COLUMNS
    scores = scores + jnp.arange(COLUMNS, dtype=jnp.int32)
    order = jnp.argsort(scores, axis=-1)[..., :SLOTS].astype(jnp.int32)
    section_part = order // PANELS_DEV
    within = order % PANELS_DEV
    rep_ids = jnp.arange(REPS, dtype=jnp.int32)[None, :, None]
    return ((section_part * REPS + rep_ids) * PANELS_DEV + within).astype(jnp.int32)


def draw_block_counts(key, part):
    first_key, second_key, third_key = jax.random.split(key, 3)
    section_count = PANELS // GROUP
    levels = jax.random.randint(first_key, (section_count, 1, 1), max(1, SLOTS // 4), SLOTS + 1)
    levels = jnp.broadcast_to(levels, (section_count, GROUP, REPS)).reshape(PANELS, REPS)
    counts = jax.random.randint(second_key, (PANELS, REPS), 1, levels + 1)
    forced = jax.random.randint(third_key, (), 0, PANELS)
    row_ids = jnp.arange(PANELS, dtype=jnp.int32)[:, None]
    return jnp.where(row_ids == forced, SLOTS, counts).astype(jnp.int32)


def block_scale(rng, dims, pieces, least, high):
    def one(dim, shards_of):
        draws = jax.random.uniform(jax.random.fold_in(jax.random.fold_in(rng, 6), dim), (shards_of,), jnp.float32, least / len(pieces), high / len(pieces))
        return jnp.repeat(jnp.exp(draws), dims[dim] // shards_of).reshape((-1,) + (1,) * (len(dims) - dim - 1))

    factor_of = one(*pieces[0])
    for cut in pieces[1:]:
        factor_of = factor_of * one(*cut)
    return factor_of


def gaussian(key, shape, width, most, cuts=(), kind=jnp.bfloat16):
    gain = block_scale(key, shape, cuts, -0.22, 0.18) if cuts else 1.0
    result = jax.random.normal(key, shape, jnp.float32) * width * gain
    return jnp.minimum(jnp.maximum(result, -most), most).astype(kind)


def setup_inputs(seed: int = 0) -> dict:
    key_of = jax.random.split(jax.random.key(seed), 8)
    features = gaussian(key_of[0], (NODES, WIDTH), 1.0, 6.0, ((0, 512),))
    col_panels = draw_col_panels(jax.random.fold_in(key_of[7], 71), 0)
    block_counts = draw_block_counts(jax.random.fold_in(key_of[7], 71), 0)
    block_values = jnp.clip(jnp.exp(math.log(0.019897461) - 2.2979944 * jax.random.uniform(key_of[3], (PANELS, REPS, SLOTS, BLOCK, BLOCK), jnp.float32) ** block_scale(key_of[3], (PANELS, REPS, SLOTS, BLOCK, BLOCK), ((0, 64), (1, 8)), -0.2, 0.2)), 0.0019989014, 0.019897461).astype(jnp.bfloat16)
    weight = gaussian(key_of[4], (WIDTH, WIDTH), WIDTH ** -0.5, 0.25)
    bias = gaussian(key_of[5], (WIDTH,), 0.5, 3.0, (), jnp.float32)
    cotangent = gaussian(key_of[6], (NODES, WIDTH), 1.0, 6.0, ((0, 512),))
    return dict(features=features, col_panels=col_panels, block_counts=block_counts, block_values=block_values, weight=weight, bias=bias, cotangent=cotangent)


def reference(features, col_panels, block_counts, block_values, weight, bias, cotangent):
    panel_feats = features.reshape(PANELS, BLOCK, WIDTH)
    slot_ids = jnp.arange(SLOTS, dtype=jnp.int32)

    def one_row(panel):
        column_ids = col_panels[panel].reshape(-1).astype(jnp.int32)
        live = (slot_ids[None, :] < block_counts[panel][:, None]).reshape(-1)
        tiles = block_values[panel].reshape(REPS * SLOTS, BLOCK, BLOCK).astype(jnp.float32)
        tiles = tiles * live[:, None, None].astype(jnp.float32)
        picked = panel_feats[column_ids].astype(jnp.float32)
        return jnp.einsum('kab,kbf->af', tiles, picked, precision=lax.Precision.HIGHEST)
    rows = lax.map(one_row, jnp.arange(PANELS, dtype=jnp.int32))
    aggregated = rows.reshape(NODES, WIDTH).astype(jnp.bfloat16)
    pre = jnp.dot(aggregated, weight, preferred_element_type=jnp.float32) + bias
    hidden = jax.nn.silu(pre).astype(jnp.bfloat16)
    sigmoid_pre = jax.nn.sigmoid(pre)
    slope = (cotangent.astype(jnp.float32) * (sigmoid_pre * (1.0 + pre * (1.0 - sigmoid_pre)))).astype(jnp.bfloat16)
    factor = 1.0 / math.sqrt(NODES)
    weight_grad = jnp.dot(aggregated.T, slope, preferred_element_type=jnp.float32) * factor
    bias_grad = lax.optimization_barrier(jnp.sum(slope.astype(jnp.float32), axis=0)) * factor
    return (hidden, weight_grad, bias_grad)
```

```python
import math

import jax
import jax.numpy as jnp
from jax import lax
from jax.sharding import Mesh
from jax.sharding import PartitionSpec as P

SECTION_AXES = ("y_hi", "z", "x")
REP_AXES = ("y_lo", "core")
ALL_AXES = SECTION_AXES + REP_AXES


def _shift_perm(n, k):
    return [(i, (i + k) % n) for i in range(n)]


def _reduce_scatter(blocks, axis, n):
    me = lax.axis_index(axis)
    acc = lax.dynamic_index_in_dim(blocks, me, 0, keepdims=False)
    for k in range(1, n):
        send = lax.dynamic_index_in_dim(blocks, (me + k) % n, 0, keepdims=False)
        acc = acc + lax.ppermute(send, axis, _shift_perm(n, k))
    return acc


def _all_gather(piece, axis, n):
    me = lax.axis_index(axis)
    pieces = [piece] + [lax.ppermute(piece, axis, _shift_perm(n, k)) for k in range(1, n)]
    stacked = jnp.stack(pieces)
    order = (me - jnp.arange(n, dtype=jnp.int32)) % n
    return jnp.take(stacked, order, axis=0)


def _all_reduce_direct(piece, axes, n):
    gathered = _all_gather(piece, axes, n)
    total = gathered[0]
    for j in range(1, n):
        total = total + gathered[j]
    return total


def shards(features, col_panels, block_counts, block_values, weight, bias, cotangent):
    sizes = {name: lax.axis_size(name) for name in ALL_AXES}
    rep_count = sizes["y_lo"] * sizes["core"]
    tile_size = block_values.shape[-1]
    feat_width = features.shape[1]
    own_panels = features.shape[0] // tile_size
    row_panels = col_panels.shape[0]
    slot_count = col_panels.shape[2]
    global_cols = col_panels[:, 0, :]
    section_of = global_cols // (own_panels * rep_count)
    low = sizes["z"] * sizes["x"]
    gathered_pos = (section_of % low) * sizes["y_hi"] + section_of // low
    local_cols = gathered_pos * own_panels + global_cols % own_panels
    live_counts = block_counts[:, 0]
    slot_mask = jnp.arange(slot_count, dtype=jnp.int32)[None, :] < live_counts[:, None]
    tiles = block_values[:, 0]
    empty = jnp.zeros((row_panels, tile_size, feat_width), jnp.float32)
    gathered = lax.all_gather(features, "y_hi", axis=0, tiled=True)
    gathered = lax.all_gather(gathered, ("z", "x"), axis=0, tiled=True)
    all_panels = gathered.reshape(-1, tile_size, feat_width)
    slot_step = 4
    turn_count = (jnp.max(live_counts) + slot_step - 1) // slot_step

    def one_turn(turn, running):
        begin_slot = turn * slot_step
        step_cols = lax.dynamic_slice_in_dim(local_cols, begin_slot, slot_step, 1)
        step_mask = lax.dynamic_slice_in_dim(slot_mask, begin_slot, slot_step, 1)
        step_tiles = lax.dynamic_slice_in_dim(tiles, begin_slot, slot_step, 1)
        step_tiles = jnp.where(step_mask[:, :, None, None], step_tiles, jnp.zeros((), jnp.bfloat16))
        picked = all_panels[step_cols]
        return running + jnp.einsum(
            "gkab,gkbf->gaf", step_tiles, picked, preferred_element_type=jnp.float32
        )

    gathered_sum = lax.fori_loop(0, turn_count, one_turn, empty)
    cores = sizes["core"]
    by_core = gathered_sum.reshape(row_panels // cores, cores, tile_size, feat_width)
    by_core = jnp.moveaxis(by_core, 1, 0)
    half = _reduce_scatter(by_core, "core", cores)
    summed_own = _reduce_scatter(half, "y_lo", sizes["y_lo"])
    own_rows = own_panels * tile_size
    aggregated = summed_own.reshape(own_rows, feat_width).astype(jnp.bfloat16)
    pre = jnp.dot(aggregated, weight, preferred_element_type=jnp.float32) + bias
    hidden = jax.nn.silu(pre).astype(jnp.bfloat16)
    sigmoid_pre = jax.nn.sigmoid(pre)
    slope = (
        cotangent.astype(jnp.float32) * (sigmoid_pre * (1.0 + pre * (1.0 - sigmoid_pre)))
    ).astype(jnp.bfloat16)
    local_weight = jnp.einsum("nd,nf->df", aggregated, slope, preferred_element_type=jnp.float32)
    local_bias = jnp.sum(slope.astype(jnp.float32), axis=0)
    width = weight.shape[0]
    scatter_ways = sizes["core"] * sizes["x"] * sizes["y_lo"]
    padded_rows = -(-(width + 1) // scatter_ways) * scatter_ways
    combined = jnp.zeros((padded_rows, feat_width), jnp.float32)
    combined = combined.at[:width].set(local_weight).at[width].set(local_bias)
    chunk = combined
    for name in ("core", "x", "y_lo"):
        chunk = _reduce_scatter(chunk.reshape(sizes[name], -1, feat_width), name, sizes[name])
    outer = sizes["z"] * sizes["y_hi"]
    chunk = _all_reduce_direct(chunk, ("y_hi", "z"), outer)
    for name in ("y_lo", "x", "core"):
        chunk = _all_gather(chunk, name, sizes[name]).reshape(-1, feat_width)
    node_total = lax.axis_size(SECTION_AXES) * rep_count * own_rows
    factor = 1.0 / math.sqrt(node_total)
    weight_sum = chunk[:width]
    bias_sum = chunk[width]
    return (hidden, weight_sum * factor, bias_sum * factor)


def solution(mesh):
    section_size, rep_size = mesh.devices.shape
    fine = Mesh(mesh.devices.reshape(2, section_size // 8, 4, rep_size // 2, 2), ALL_AXES)
    in_specs = (
        P(ALL_AXES, None),
        P(SECTION_AXES, REP_AXES, None),
        P(SECTION_AXES, REP_AXES),
        P(SECTION_AXES, REP_AXES, None, None, None),
        P(),
        P(),
        P(ALL_AXES, None),
    )
    out_specs = (P(ALL_AXES, None), P(), P())
    return jax.shard_map(shards, mesh=fine, in_specs=in_specs, out_specs=out_specs, check_vma=False)
```

```python
import math

import jax
import jax.numpy as jnp
from jax import lax
from jax.sharding import Mesh
from jax.sharding import PartitionSpec as P

SECTION_AXES = ("y_hi", "z", "x")
REP_AXES = ("y_lo", "core")
ALL_AXES = SECTION_AXES + REP_AXES


def _xor_perm(n, bit):
    return [(i, i ^ bit) for i in range(n)]


def _halving_scatter(blocks, axis, n):
    me = lax.axis_index(axis)
    bit = n // 2
    while bit >= 1:
        pairs = blocks.reshape((2, blocks.shape[0] // 2) + blocks.shape[1:])
        mine = (me // bit) % 2
        keep = lax.dynamic_index_in_dim(pairs, mine, 0, keepdims=False)
        send = lax.dynamic_index_in_dim(pairs, 1 - mine, 0, keepdims=False)
        blocks = keep + lax.ppermute(send, axis, _xor_perm(n, bit))
        bit //= 2
    return blocks[0]


def _doubling_gather(piece, axis, n):
    me = lax.axis_index(axis)
    bit = 1
    while bit < n:
        other = lax.ppermute(piece, axis, _xor_perm(n, bit))
        upper = (me // bit) % 2 == 1
        low = jnp.where(upper, other, piece)
        high = jnp.where(upper, piece, other)
        piece = jnp.concatenate([low, high], axis=0)
        bit *= 2
    return piece


def _doubling_sum(piece, axis, n):
    bit = 1
    while bit < n:
        piece = piece + lax.ppermute(piece, axis, _xor_perm(n, bit))
        bit *= 2
    return piece


def shards(features, col_panels, block_counts, block_values, weight, bias, cotangent):
    sizes = {name: lax.axis_size(name) for name in ALL_AXES}
    rep_count = sizes["y_lo"] * sizes["core"]
    tile_size = block_values.shape[-1]
    feat_width = features.shape[1]
    own_panels = features.shape[0] // tile_size
    row_panels = col_panels.shape[0]
    slot_count = col_panels.shape[2]
    global_cols = col_panels[:, 0, :]
    section_of = global_cols // (own_panels * rep_count)
    low = sizes["z"] * sizes["x"]
    gathered_pos = (section_of % low) * sizes["y_hi"] + section_of // low
    local_cols = gathered_pos * own_panels + global_cols % own_panels
    live_counts = block_counts[:, 0]
    slot_mask = jnp.arange(slot_count, dtype=jnp.int32)[None, :] < live_counts[:, None]
    tiles = block_values[:, 0]
    empty = jnp.zeros((row_panels, tile_size, feat_width), jnp.float32)
    gathered = lax.all_gather(features, "y_hi", axis=0, tiled=True)
    gathered = lax.all_gather(gathered, ("z", "x"), axis=0, tiled=True)
    all_panels = gathered.reshape(-1, tile_size, feat_width)
    slot_step = 4
    turn_count = (jnp.max(live_counts) + slot_step - 1) // slot_step

    def one_turn(turn, running):
        begin_slot = turn * slot_step
        step_cols = lax.dynamic_slice_in_dim(local_cols, begin_slot, slot_step, 1)
        step_mask = lax.dynamic_slice_in_dim(slot_mask, begin_slot, slot_step, 1)
        step_tiles = lax.dynamic_slice_in_dim(tiles, begin_slot, slot_step, 1)
        step_tiles = jnp.where(step_mask[:, :, None, None], step_tiles, jnp.zeros((), jnp.bfloat16))
        picked = all_panels[step_cols]
        return running + jnp.einsum(
            "gkab,gkbf->gaf", step_tiles, picked, preferred_element_type=jnp.float32
        )

    gathered_sum = lax.fori_loop(0, turn_count, one_turn, empty)
    cores = sizes["core"]
    by_core = gathered_sum.reshape(row_panels // cores, cores, tile_size, feat_width)
    by_core = jnp.moveaxis(by_core, 1, 0)
    half = _halving_scatter(by_core, "core", cores)
    summed_own = _halving_scatter(half.reshape((sizes["y_lo"], 1) + half.shape[1:]), "y_lo", sizes["y_lo"])
    own_rows = own_panels * tile_size
    aggregated = summed_own.reshape(own_rows, feat_width).astype(jnp.bfloat16)
    pre = jnp.dot(aggregated, weight, preferred_element_type=jnp.float32) + bias
    hidden = jax.nn.silu(pre).astype(jnp.bfloat16)
    sigmoid_pre = jax.nn.sigmoid(pre)
    slope = (
        cotangent.astype(jnp.float32) * (sigmoid_pre * (1.0 + pre * (1.0 - sigmoid_pre)))
    ).astype(jnp.bfloat16)
    local_weight = jnp.einsum("nd,nf->df", aggregated, slope, preferred_element_type=jnp.float32)
    local_bias = jnp.sum(slope.astype(jnp.float32), axis=0)
    width = weight.shape[0]
    scatter_ways = sizes["core"] * sizes["x"]
    padded_rows = -(-(width + 1) // (scatter_ways * 8)) * scatter_ways * 8
    combined = jnp.zeros((padded_rows, feat_width), jnp.float32)
    combined = combined.at[:width].set(local_weight).at[width].set(local_bias)
    chunk = _halving_scatter(combined.reshape(sizes["core"], -1, feat_width), "core", sizes["core"])
    chunk = _halving_scatter(chunk.reshape(sizes["x"], -1, feat_width), "x", sizes["x"])
    for name in ("y_lo", "z", "y_hi"):
        chunk = _doubling_sum(chunk, name, sizes[name])
    chunk = _doubling_gather(chunk, "x", sizes["x"])
    chunk = _doubling_gather(chunk, "core", sizes["core"])
    node_total = lax.axis_size(SECTION_AXES) * rep_count * own_rows
    factor = 1.0 / math.sqrt(node_total)
    weight_sum = chunk[:width]
    bias_sum = chunk[width]
    return (hidden, weight_sum * factor, bias_sum * factor)


def solution(mesh):
    section_size, rep_size = mesh.devices.shape
    fine = Mesh(mesh.devices.reshape(2, section_size // 8, 4, rep_size // 2, 2), ALL_AXES)
    in_specs = (
        P(ALL_AXES, None),
        P(SECTION_AXES, REP_AXES, None),
        P(SECTION_AXES, REP_AXES),
        P(SECTION_AXES, REP_AXES, None, None, None),
        P(),
        P(),
        P(ALL_AXES, None),
    )
    out_specs = (P(ALL_AXES, None), P(), P())
    return jax.shard_map(shards, mesh=fine, in_specs=in_specs, out_specs=out_specs, check_vma=False)
```

```python
import math

import jax
import jax.numpy as jnp
from jax import lax
from jax.experimental import pallas as pl
from jax.experimental.pallas import tpu as pltpu
from jax.sharding import Mesh
from jax.sharding import PartitionSpec as P

SECTION_AXES = ("y_hi", "z", "x")
REP_AXES = ("y_lo", "core")
ALL_AXES = SECTION_AXES + REP_AXES


def _xor_perm(n, bit):
    return [(i, i ^ bit) for i in range(n)]


def _halving_scatter(blocks, axis, n):
    me = lax.axis_index(axis)
    bit = n // 2
    while bit >= 1:
        pairs = blocks.reshape((2, blocks.shape[0] // 2) + blocks.shape[1:])
        mine = (me // bit) % 2
        keep = lax.dynamic_index_in_dim(pairs, mine, 0, keepdims=False)
        send = lax.dynamic_index_in_dim(pairs, 1 - mine, 0, keepdims=False)
        blocks = keep + lax.ppermute(send, axis, _xor_perm(n, bit))
        bit //= 2
    return blocks[0]


def _doubling_gather(piece, axis, n):
    me = lax.axis_index(axis)
    bit = 1
    while bit < n:
        other = lax.ppermute(piece, axis, _xor_perm(n, bit))
        upper = (me // bit) % 2 == 1
        low = jnp.where(upper, other, piece)
        high = jnp.where(upper, piece, other)
        piece = jnp.concatenate([low, high], axis=0)
        bit *= 2
    return piece


def _doubling_sum(piece, axis, n):
    bit = 1
    while bit < n:
        piece = piece + lax.ppermute(piece, axis, _xor_perm(n, bit))
        bit *= 2
    return piece


def _aggregate_kernel(cols_ref, counts_ref, tiles_ref, panels_ref, out_ref):
    groups, slots = tiles_ref.shape[0], tiles_ref.shape[1]
    for g in range(groups):
        out_ref[g] = jnp.zeros(out_ref.shape[1:], jnp.float32)

        def body(k, carry, g=g):
            col = cols_ref[g * slots + k]
            out_ref[g] += jnp.dot(tiles_ref[g, k], panels_ref[col], preferred_element_type=jnp.float32)
            return carry

        lax.fori_loop(0, counts_ref[g], body, 0)


def _aggregate(cols, counts, tiles, panels):
    groups, slots, tile_size, _ = tiles.shape
    feat_width = panels.shape[-1]
    flops = 2 * groups * slots * tile_size * tile_size * feat_width
    moved = tiles.size * 2 + panels.size * 2 + groups * tile_size * feat_width * 4
    return pl.pallas_call(
        _aggregate_kernel,
        out_shape=jax.ShapeDtypeStruct((groups, tile_size, feat_width), jnp.float32),
        in_specs=[
            pl.BlockSpec(memory_space=pltpu.SMEM),
            pl.BlockSpec(memory_space=pltpu.SMEM),
            pl.BlockSpec(memory_space=pltpu.VMEM),
            pl.BlockSpec(memory_space=pltpu.VMEM),
        ],
        out_specs=pl.BlockSpec(memory_space=pltpu.VMEM),
        cost_estimate=pl.CostEstimate(flops=flops, bytes_accessed=moved, transcendentals=0),
    )(
        jnp.clip(cols, 0, panels.shape[0] - 1).reshape(-1),
        jnp.clip(counts, 0, slots),
        tiles,
        panels,
    )


def shards(features, col_panels, block_counts, block_values, weight, bias, cotangent):
    sizes = {name: lax.axis_size(name) for name in ALL_AXES}
    rep_count = sizes["y_lo"] * sizes["core"]
    tile_size = block_values.shape[-1]
    feat_width = features.shape[1]
    own_panels = features.shape[0] // tile_size
    row_panels = col_panels.shape[0]
    global_cols = col_panels[:, 0, :]
    section_of = global_cols // (own_panels * rep_count)
    low = sizes["z"] * sizes["x"]
    gathered_pos = (section_of % low) * sizes["y_hi"] + section_of // low
    local_cols = gathered_pos * own_panels + global_cols % own_panels
    live_counts = block_counts[:, 0]
    tiles = block_values[:, 0]
    gathered = lax.all_gather(features, "y_hi", axis=0, tiled=True)
    gathered = lax.all_gather(gathered, ("z", "x"), axis=0, tiled=True)
    all_panels = gathered.reshape(-1, tile_size, feat_width)
    gathered_sum = _aggregate(local_cols, live_counts, tiles, all_panels)
    cores = sizes["core"]
    by_core = gathered_sum.reshape(row_panels // cores, cores, tile_size, feat_width)
    by_core = jnp.moveaxis(by_core, 1, 0)
    half = _halving_scatter(by_core, "core", cores)
    summed_own = _halving_scatter(half.reshape((sizes["y_lo"], 1) + half.shape[1:]), "y_lo", sizes["y_lo"])
    own_rows = own_panels * tile_size
    aggregated = summed_own.reshape(own_rows, feat_width).astype(jnp.bfloat16)
    pre = jnp.dot(aggregated, weight, preferred_element_type=jnp.float32) + bias
    hidden = jax.nn.silu(pre).astype(jnp.bfloat16)
    sigmoid_pre = jax.nn.sigmoid(pre)
    slope = (
        cotangent.astype(jnp.float32) * (sigmoid_pre * (1.0 + pre * (1.0 - sigmoid_pre)))
    ).astype(jnp.bfloat16)
    local_weight = jnp.einsum("nd,nf->df", aggregated, slope, preferred_element_type=jnp.float32)
    local_bias = jnp.sum(slope.astype(jnp.float32), axis=0)
    width = weight.shape[0]
    scatter_ways = sizes["core"] * sizes["x"]
    padded_rows = -(-(width + 1) // (scatter_ways * 8)) * scatter_ways * 8
    combined = jnp.zeros((padded_rows, feat_width), jnp.float32)
    combined = combined.at[:width].set(local_weight).at[width].set(local_bias)
    chunk = _halving_scatter(combined.reshape(sizes["core"], -1, feat_width), "core", sizes["core"])
    chunk = _halving_scatter(chunk.reshape(sizes["x"], -1, feat_width), "x", sizes["x"])
    for name in ("y_lo", "z", "y_hi"):
        chunk = _doubling_sum(chunk, name, sizes[name])
    chunk = _doubling_gather(chunk, "x", sizes["x"])
    chunk = _doubling_gather(chunk, "core", sizes["core"])
    node_total = lax.axis_size(SECTION_AXES) * rep_count * own_rows
    factor = 1.0 / math.sqrt(node_total)
    weight_sum = chunk[:width]
    bias_sum = chunk[width]
    return (hidden, weight_sum * factor, bias_sum * factor)


def solution(mesh):
    section_size, rep_size = mesh.devices.shape
    fine = Mesh(mesh.devices.reshape(2, section_size // 8, 4, rep_size // 2, 2), ALL_AXES)
    in_specs = (
        P(ALL_AXES, None),
        P(SECTION_AXES, REP_AXES, None),
        P(SECTION_AXES, REP_AXES),
        P(SECTION_AXES, REP_AXES, None, None, None),
        P(),
        P(),
        P(ALL_AXES, None),
    )
    out_specs = (P(ALL_AXES, None), P(), P())
    return jax.shard_map(shards, mesh=fine, in_specs=in_specs, out_specs=out_specs, check_vma=False)
```

```python
import math

import jax
import jax.numpy as jnp
from jax import lax
from jax.experimental import pallas as pl
from jax.experimental.pallas import tpu as pltpu
from jax.sharding import Mesh
from jax.sharding import PartitionSpec as P

SECTION_AXES = ("y_hi", "z", "x")
REP_AXES = ("y_lo", "core")
ALL_AXES = SECTION_AXES + REP_AXES


def _xor_perm(n, bit):
    return [(i, i ^ bit) for i in range(n)]


def _halving_scatter(blocks, axis, n):
    me = lax.axis_index(axis)
    bit = n // 2
    while bit >= 1:
        pairs = blocks.reshape((2, blocks.shape[0] // 2) + blocks.shape[1:])
        mine = (me // bit) % 2
        keep = lax.dynamic_index_in_dim(pairs, mine, 0, keepdims=False)
        send = lax.dynamic_index_in_dim(pairs, 1 - mine, 0, keepdims=False)
        blocks = keep + lax.ppermute(send, axis, _xor_perm(n, bit))
        bit //= 2
    return blocks[0]


def _doubling_gather(piece, axis, n):
    me = lax.axis_index(axis)
    bit = 1
    while bit < n:
        other = lax.ppermute(piece, axis, _xor_perm(n, bit))
        upper = (me // bit) % 2 == 1
        low = jnp.where(upper, other, piece)
        high = jnp.where(upper, piece, other)
        piece = jnp.concatenate([low, high], axis=0)
        bit *= 2
    return piece


def _doubling_sum(piece, axis, n):
    bit = 1
    while bit < n:
        piece = piece + lax.ppermute(piece, axis, _xor_perm(n, bit))
        bit *= 2
    return piece


def _aggregate_kernel(cols_ref, tiles_ref, panels_hbm, out_ref, buf, sems):
    groups, slots = out_ref.shape[0], buf.shape[1]

    def copies(g, slot):
        return [
            pltpu.make_async_copy(panels_hbm.at[cols_ref[g * slots + k]], buf.at[slot, k], sems.at[slot, k])
            for k in range(slots)
        ]

    pending = copies(0, 0)
    for c in pending:
        c.start()
    for g in range(groups):
        slot = g % 2
        if g + 1 < groups:
            ahead = copies(g + 1, 1 - slot)
            for c in ahead:
                c.start()
        for c in pending:
            c.wait()
        rhs = buf[slot].reshape(slots * buf.shape[2], buf.shape[3])
        out_ref[g] = jnp.dot(tiles_ref[g], rhs, preferred_element_type=jnp.float32)
        if g + 1 < groups:
            pending = ahead


def _aggregate(cols, counts, tiles, panels):
    groups, slots, tile_size, _ = tiles.shape
    feat_width = panels.shape[-1]
    live = jnp.arange(slots, dtype=jnp.int32)[None, :] < counts[:, None]
    wide = jnp.where(live[:, :, None, None], tiles, jnp.zeros((), tiles.dtype))
    wide = wide.transpose(0, 2, 1, 3).reshape(groups, tile_size, slots * tile_size)
    flops = 2 * groups * slots * tile_size * tile_size * feat_width
    moved = tiles.size * 2 + groups * slots * tile_size * feat_width * 2 + groups * tile_size * feat_width * 4
    return pl.pallas_call(
        _aggregate_kernel,
        out_shape=jax.ShapeDtypeStruct((groups, tile_size, feat_width), jnp.float32),
        in_specs=[
            pl.BlockSpec(memory_space=pltpu.SMEM),
            pl.BlockSpec(memory_space=pltpu.VMEM),
            pl.BlockSpec(memory_space=pl.ANY),
        ],
        out_specs=pl.BlockSpec(memory_space=pltpu.VMEM),
        scratch_shapes=[
            pltpu.VMEM((2, slots, tile_size, feat_width), panels.dtype),
            pltpu.SemaphoreType.DMA((2, slots)),
        ],
        cost_estimate=pl.CostEstimate(flops=flops, bytes_accessed=moved, transcendentals=0),
    )(jnp.clip(cols, 0, panels.shape[0] - 1).reshape(-1), wide, panels)


def shards(features, col_panels, block_counts, block_values, weight, bias, cotangent):
    sizes = {name: lax.axis_size(name) for name in ALL_AXES}
    rep_count = sizes["y_lo"] * sizes["core"]
    tile_size = block_values.shape[-1]
    feat_width = features.shape[1]
    own_panels = features.shape[0] // tile_size
    row_panels = col_panels.shape[0]
    global_cols = col_panels[:, 0, :]
    section_of = global_cols // (own_panels * rep_count)
    low = sizes["z"] * sizes["x"]
    gathered_pos = (section_of % low) * sizes["y_hi"] + section_of // low
    local_cols = gathered_pos * own_panels + global_cols % own_panels
    live_counts = block_counts[:, 0]
    tiles = block_values[:, 0]
    gathered = lax.all_gather(features, "y_hi", axis=0, tiled=True)
    gathered = lax.all_gather(gathered, ("z", "x"), axis=0, tiled=True)
    all_panels = gathered.reshape(-1, tile_size, feat_width)
    gathered_sum = _aggregate(local_cols, live_counts, tiles, all_panels)
    cores = sizes["core"]
    by_core = gathered_sum.reshape(row_panels // cores, cores, tile_size, feat_width)
    by_core = jnp.moveaxis(by_core, 1, 0)
    half = _halving_scatter(by_core, "core", cores)
    summed_own = _halving_scatter(half.reshape((sizes["y_lo"], 1) + half.shape[1:]), "y_lo", sizes["y_lo"])
    own_rows = own_panels * tile_size
    aggregated = summed_own.reshape(own_rows, feat_width).astype(jnp.bfloat16)
    pre = jnp.dot(aggregated, weight, preferred_element_type=jnp.float32) + bias
    hidden = jax.nn.silu(pre).astype(jnp.bfloat16)
    sigmoid_pre = jax.nn.sigmoid(pre)
    slope = (
        cotangent.astype(jnp.float32) * (sigmoid_pre * (1.0 + pre * (1.0 - sigmoid_pre)))
    ).astype(jnp.bfloat16)
    local_weight = jnp.einsum("nd,nf->df", aggregated, slope, preferred_element_type=jnp.float32)
    local_bias = jnp.sum(slope.astype(jnp.float32), axis=0)
    width = weight.shape[0]
    scatter_ways = sizes["core"] * sizes["x"]
    padded_rows = -(-(width + 1) // (scatter_ways * 8)) * scatter_ways * 8
    combined = jnp.zeros((padded_rows, feat_width), jnp.float32)
    combined = combined.at[:width].set(local_weight).at[width].set(local_bias)
    chunk = _halving_scatter(combined.reshape(sizes["core"], -1, feat_width), "core", sizes["core"])
    chunk = _halving_scatter(chunk.reshape(sizes["x"], -1, feat_width), "x", sizes["x"])
    for name in ("y_lo", "z", "y_hi"):
        chunk = _doubling_sum(chunk, name, sizes[name])
    chunk = _doubling_gather(chunk, "x", sizes["x"])
    chunk = _doubling_gather(chunk, "core", sizes["core"])
    node_total = lax.axis_size(SECTION_AXES) * rep_count * own_rows
    factor = 1.0 / math.sqrt(node_total)
    weight_sum = chunk[:width]
    bias_sum = chunk[width]
    return (hidden, weight_sum * factor, bias_sum * factor)


def solution(mesh):
    section_size, rep_size = mesh.devices.shape
    fine = Mesh(mesh.devices.reshape(2, section_size // 8, 4, rep_size // 2, 2), ALL_AXES)
    in_specs = (
        P(ALL_AXES, None),
        P(SECTION_AXES, REP_AXES, None),
        P(SECTION_AXES, REP_AXES),
        P(SECTION_AXES, REP_AXES, None, None, None),
        P(),
        P(),
        P(ALL_AXES, None),
    )
    out_specs = (P(ALL_AXES, None), P(), P())
    return jax.shard_map(shards, mesh=fine, in_specs=in_specs, out_specs=out_specs, check_vma=False)
```

```python
import math

import jax
import jax.numpy as jnp
from jax import lax
from jax.experimental import pallas as pl
from jax.experimental.pallas import tpu as pltpu
from jax.sharding import Mesh
from jax.sharding import PartitionSpec as P

SECTION_AXES = ("y_hi", "z", "x")
REP_AXES = ("y_lo", "core")
ALL_AXES = SECTION_AXES + REP_AXES


def _xor_perm(n, bit):
    return [(i, i ^ bit) for i in range(n)]


def _halving_scatter(blocks, axis, n, bits):
    me = lax.axis_index(axis)
    depth = n.bit_length() - 1
    rest = blocks.shape[1:]
    blocks = blocks.reshape((2,) * depth + rest)
    left = list(range(depth - 1, -1, -1))
    for bit in bits:
        at = left.index(bit)
        mine = (me // (1 << bit)) % 2
        keep = lax.dynamic_index_in_dim(blocks, mine, at, keepdims=False)
        send = lax.dynamic_index_in_dim(blocks, 1 - mine, at, keepdims=False)
        blocks = keep + lax.ppermute(send, axis, _xor_perm(n, 1 << bit))
        left.pop(at)
    return blocks


def _doubling_gather(piece, axis, n, bits):
    me = lax.axis_index(axis)
    rest = piece.shape
    got = []
    for bit in bits:
        other = lax.ppermute(piece, axis, _xor_perm(n, 1 << bit))
        upper = (me // (1 << bit)) % 2 == 1
        low = jnp.where(upper, other, piece)
        high = jnp.where(upper, piece, other)
        piece = jnp.stack([low, high])
        got = [bit] + got
    order = sorted(range(len(got)), key=lambda i: -got[i])
    piece = jnp.transpose(piece, order + list(range(len(got), piece.ndim)))
    return piece.reshape((n * rest[0],) + rest[1:])


def _doubling_sum(piece, axis, n):
    bit = 1
    while bit < n:
        piece = piece + lax.ppermute(piece, axis, _xor_perm(n, bit))
        bit *= 2
    return piece


def _aggregate_kernel(cols_ref, tiles_ref, panels_hbm, out_ref, buf, sems):
    groups, slots = out_ref.shape[0], buf.shape[1]

    def copies(g, slot):
        return [
            pltpu.make_async_copy(panels_hbm.at[cols_ref[g * slots + k]], buf.at[slot, k], sems.at[slot, k])
            for k in range(slots)
        ]

    pending = copies(0, 0)
    for c in pending:
        c.start()
    for g in range(groups):
        slot = g % 2
        if g + 1 < groups:
            ahead = copies(g + 1, 1 - slot)
            for c in ahead:
                c.start()
        for c in pending:
            c.wait()
        rhs = buf[slot].reshape(slots * buf.shape[2], buf.shape[3])
        out_ref[g] = jnp.dot(tiles_ref[g], rhs, preferred_element_type=jnp.float32)
        if g + 1 < groups:
            pending = ahead


def _aggregate(cols, counts, tiles, panels):
    groups, slots, tile_size, _ = tiles.shape
    feat_width = panels.shape[-1]
    live = jnp.arange(slots, dtype=jnp.int32)[None, :] < counts[:, None]
    wide = jnp.where(live[:, :, None, None], tiles, jnp.zeros((), tiles.dtype))
    wide = wide.transpose(0, 2, 1, 3).reshape(groups, tile_size, slots * tile_size)
    flops = 2 * groups * slots * tile_size * tile_size * feat_width
    moved = tiles.size * 2 + groups * slots * tile_size * feat_width * 2 + groups * tile_size * feat_width * 4
    return pl.pallas_call(
        _aggregate_kernel,
        out_shape=jax.ShapeDtypeStruct((groups, tile_size, feat_width), jnp.float32),
        in_specs=[
            pl.BlockSpec(memory_space=pltpu.SMEM),
            pl.BlockSpec(memory_space=pltpu.VMEM),
            pl.BlockSpec(memory_space=pl.ANY),
        ],
        out_specs=pl.BlockSpec(memory_space=pltpu.VMEM),
        scratch_shapes=[
            pltpu.VMEM((2, slots, tile_size, feat_width), panels.dtype),
            pltpu.SemaphoreType.DMA((2, slots)),
        ],
        cost_estimate=pl.CostEstimate(flops=flops, bytes_accessed=moved, transcendentals=0),
    )(jnp.clip(cols, 0, panels.shape[0] - 1).reshape(-1), wide, panels)


def shards(features, col_panels, block_counts, block_values, weight, bias, cotangent):
    sizes = {name: lax.axis_size(name) for name in ALL_AXES}
    rep_count = sizes["y_lo"] * sizes["core"]
    tile_size = block_values.shape[-1]
    feat_width = features.shape[1]
    own_panels = features.shape[0] // tile_size
    row_panels = col_panels.shape[0]
    global_cols = col_panels[:, 0, :]
    section_of = global_cols // (own_panels * rep_count)
    low = sizes["z"] * sizes["x"]
    gathered_pos = (section_of % low) * sizes["y_hi"] + section_of // low
    local_cols = gathered_pos * own_panels + global_cols % own_panels
    live_counts = block_counts[:, 0]
    tiles = block_values[:, 0]
    gathered = lax.all_gather(features, "y_hi", axis=0, tiled=True)
    gathered = lax.all_gather(gathered, ("z", "x"), axis=0, tiled=True)
    all_panels = gathered.reshape(-1, tile_size, feat_width)
    gathered_sum = _aggregate(local_cols, live_counts, tiles, all_panels)
    cores = sizes["core"]
    by_core = gathered_sum.reshape(row_panels // cores, cores, tile_size, feat_width)
    by_core = jnp.moveaxis(by_core, 1, 0)
    half = _halving_scatter(by_core, "core", cores, (0,))
    summed_own = _halving_scatter(half, "y_lo", sizes["y_lo"], (0, 1))
    own_rows = own_panels * tile_size
    aggregated = summed_own.reshape(own_rows, feat_width).astype(jnp.bfloat16)
    pre = jnp.dot(aggregated, weight, preferred_element_type=jnp.float32) + bias
    hidden = jax.nn.silu(pre).astype(jnp.bfloat16)
    sigmoid_pre = jax.nn.sigmoid(pre)
    slope = (
        cotangent.astype(jnp.float32) * (sigmoid_pre * (1.0 + pre * (1.0 - sigmoid_pre)))
    ).astype(jnp.bfloat16)
    local_weight = jnp.einsum("nd,nf->df", aggregated, slope, preferred_element_type=jnp.float32)
    local_bias = jnp.sum(slope.astype(jnp.float32), axis=0)
    width = weight.shape[0]
    scatter_ways = sizes["core"] * sizes["x"]
    padded_rows = -(-(width + 1) // (scatter_ways * 8)) * scatter_ways * 8
    combined = jnp.zeros((padded_rows, feat_width), jnp.float32)
    combined = combined.at[:width].set(local_weight).at[width].set(local_bias)
    chunk = _halving_scatter(combined.reshape(sizes["core"], -1, feat_width), "core", sizes["core"], (0,))
    chunk = _halving_scatter(chunk.reshape(sizes["x"], -1, feat_width), "x", sizes["x"], (0, 1))
    for name in ("y_lo", "z", "y_hi"):
        chunk = _doubling_sum(chunk, name, sizes[name])
    chunk = _doubling_gather(chunk, "x", sizes["x"], (1, 0))
    chunk = _doubling_gather(chunk, "core", sizes["core"], (0,))
    node_total = lax.axis_size(SECTION_AXES) * rep_count * own_rows
    factor = 1.0 / math.sqrt(node_total)
    weight_sum = chunk[:width]
    bias_sum = chunk[width]
    return (hidden, weight_sum * factor, bias_sum * factor)


def solution(mesh):
    section_size, rep_size = mesh.devices.shape
    fine = Mesh(mesh.devices.reshape(2, section_size // 8, 4, rep_size // 2, 2), ALL_AXES)
    in_specs = (
        P(ALL_AXES, None),
        P(SECTION_AXES, REP_AXES, None),
        P(SECTION_AXES, REP_AXES),
        P(SECTION_AXES, REP_AXES, None, None, None),
        P(),
        P(),
        P(ALL_AXES, None),
    )
    out_specs = (P(ALL_AXES, None), P(), P())
    return jax.shard_map(shards, mesh=fine, in_specs=in_specs, out_specs=out_specs, check_vma=False)
```

```python
import math

import jax
import jax.numpy as jnp
from jax import lax
from jax.experimental import pallas as pl
from jax.experimental.pallas import tpu as pltpu
from jax.sharding import Mesh
from jax.sharding import PartitionSpec as P

SECTION_AXES = ("y_hi", "z", "x")
REP_AXES = ("y_lo", "core")
ALL_AXES = SECTION_AXES + REP_AXES


def _xor_perm(n, bit):
    return [(i, i ^ bit) for i in range(n)]


def _halving_scatter(blocks, axis, n, bits, wire=None):
    me = lax.axis_index(axis)
    depth = n.bit_length() - 1
    rest = blocks.shape[1:]
    blocks = blocks.reshape((2,) * depth + rest)
    left = list(range(depth - 1, -1, -1))
    for bit in bits:
        at = left.index(bit)
        mine = (me // (1 << bit)) % 2
        keep = lax.dynamic_index_in_dim(blocks, mine, at, keepdims=False)
        send = lax.dynamic_index_in_dim(blocks, 1 - mine, at, keepdims=False)
        if wire is not None:
            send = send.astype(wire)
        blocks = keep + lax.ppermute(send, axis, _xor_perm(n, 1 << bit)).astype(keep.dtype)
        left.pop(at)
    return blocks


def _doubling_gather(piece, axis, n, bits):
    me = lax.axis_index(axis)
    rest = piece.shape
    got = []
    for bit in bits:
        other = lax.ppermute(piece, axis, _xor_perm(n, 1 << bit))
        upper = (me // (1 << bit)) % 2 == 1
        low = jnp.where(upper, other, piece)
        high = jnp.where(upper, piece, other)
        piece = jnp.stack([low, high])
        got = [bit] + got
    order = sorted(range(len(got)), key=lambda i: -got[i])
    piece = jnp.transpose(piece, order + list(range(len(got), piece.ndim)))
    return piece.reshape((n * rest[0],) + rest[1:])


def _doubling_sum(piece, axis, n):
    bit = 1
    while bit < n:
        piece = piece + lax.ppermute(piece, axis, _xor_perm(n, bit))
        bit *= 2
    return piece


def _aggregate_kernel(cols_ref, tiles_ref, panels_hbm, out_ref, buf, sems):
    groups, slots = out_ref.shape[0], buf.shape[1]

    def copies(g, slot):
        return [
            pltpu.make_async_copy(panels_hbm.at[cols_ref[g * slots + k]], buf.at[slot, k], sems.at[slot, k])
            for k in range(slots)
        ]

    pending = copies(0, 0)
    for c in pending:
        c.start()
    for g in range(groups):
        slot = g % 2
        if g + 1 < groups:
            ahead = copies(g + 1, 1 - slot)
            for c in ahead:
                c.start()
        for c in pending:
            c.wait()
        rhs = buf[slot].reshape(slots * buf.shape[2], buf.shape[3])
        out_ref[g] = jnp.dot(tiles_ref[g], rhs, preferred_element_type=jnp.float32)
        if g + 1 < groups:
            pending = ahead


def _aggregate(cols, counts, tiles, panels):
    groups, slots, tile_size, _ = tiles.shape
    feat_width = panels.shape[-1]
    live = jnp.arange(slots, dtype=jnp.int32)[None, :] < counts[:, None]
    wide = jnp.where(live[:, :, None, None], tiles, jnp.zeros((), tiles.dtype))
    wide = wide.transpose(0, 2, 1, 3).reshape(groups, tile_size, slots * tile_size)
    flops = 2 * groups * slots * tile_size * tile_size * feat_width
    moved = tiles.size * 2 + groups * slots * tile_size * feat_width * 2 + groups * tile_size * feat_width * 4
    return pl.pallas_call(
        _aggregate_kernel,
        out_shape=jax.ShapeDtypeStruct((groups, tile_size, feat_width), jnp.float32),
        in_specs=[
            pl.BlockSpec(memory_space=pltpu.SMEM),
            pl.BlockSpec(memory_space=pltpu.VMEM),
            pl.BlockSpec(memory_space=pl.ANY),
        ],
        out_specs=pl.BlockSpec(memory_space=pltpu.VMEM),
        scratch_shapes=[
            pltpu.VMEM((2, slots, tile_size, feat_width), panels.dtype),
            pltpu.SemaphoreType.DMA((2, slots)),
        ],
        cost_estimate=pl.CostEstimate(flops=flops, bytes_accessed=moved, transcendentals=0),
    )(jnp.clip(cols, 0, panels.shape[0] - 1).reshape(-1), wide, panels)


def shards(features, col_panels, block_counts, block_values, weight, bias, cotangent):
    sizes = {name: lax.axis_size(name) for name in ALL_AXES}
    rep_count = sizes["y_lo"] * sizes["core"]
    tile_size = block_values.shape[-1]
    feat_width = features.shape[1]
    own_panels = features.shape[0] // tile_size
    row_panels = col_panels.shape[0]
    global_cols = col_panels[:, 0, :]
    section_of = global_cols // (own_panels * rep_count)
    low = sizes["z"] * sizes["x"]
    gathered_pos = (section_of % low) * sizes["y_hi"] + section_of // low
    local_cols = gathered_pos * own_panels + global_cols % own_panels
    live_counts = block_counts[:, 0]
    tiles = block_values[:, 0]
    gathered = lax.all_gather(features, "y_hi", axis=0, tiled=True)
    gathered = lax.all_gather(gathered, ("z", "x"), axis=0, tiled=True)
    all_panels = gathered.reshape(-1, tile_size, feat_width)
    gathered_sum = _aggregate(local_cols, live_counts, tiles, all_panels)
    cores = sizes["core"]
    by_core = gathered_sum.reshape(row_panels // cores, cores, tile_size, feat_width)
    by_core = jnp.moveaxis(by_core, 1, 0)
    half = _halving_scatter(by_core, "core", cores, (0,))
    summed_own = _halving_scatter(half, "y_lo", sizes["y_lo"], (0, 1), jnp.bfloat16)
    own_rows = own_panels * tile_size
    aggregated = summed_own.reshape(own_rows, feat_width).astype(jnp.bfloat16)
    pre = jnp.dot(aggregated, weight, preferred_element_type=jnp.float32) + bias
    hidden = jax.nn.silu(pre).astype(jnp.bfloat16)
    sigmoid_pre = jax.nn.sigmoid(pre)
    slope = (
        cotangent.astype(jnp.float32) * (sigmoid_pre * (1.0 + pre * (1.0 - sigmoid_pre)))
    ).astype(jnp.bfloat16)
    local_weight = jnp.einsum("nd,nf->df", aggregated, slope, preferred_element_type=jnp.float32)
    local_bias = jnp.sum(slope.astype(jnp.float32), axis=0)
    width = weight.shape[0]
    scatter_ways = sizes["core"] * sizes["x"] * sizes["y_lo"]
    padded_rows = -(-(width + 1) // scatter_ways) * scatter_ways
    combined = jnp.zeros((padded_rows, feat_width), jnp.float32)
    combined = combined.at[:width].set(local_weight).at[width].set(local_bias)
    chunk = combined
    for name in ("core", "x", "y_lo"):
        order = tuple(range(sizes[name].bit_length() - 1))
        chunk = _halving_scatter(chunk.reshape(sizes[name], -1, feat_width), name, sizes[name], order)
    for name in ("z", "y_hi"):
        chunk = _doubling_sum(chunk, name, sizes[name])
    for name in ("y_lo", "x", "core"):
        order = tuple(range(sizes[name].bit_length() - 2, -1, -1))
        chunk = _doubling_gather(chunk, name, sizes[name], order)
    node_total = lax.axis_size(SECTION_AXES) * rep_count * own_rows
    factor = 1.0 / math.sqrt(node_total)
    weight_sum = chunk[:width]
    bias_sum = chunk[width]
    return (hidden, weight_sum * factor, bias_sum * factor)


def solution(mesh):
    section_size, rep_size = mesh.devices.shape
    fine = Mesh(mesh.devices.reshape(2, section_size // 8, 4, rep_size // 2, 2), ALL_AXES)
    in_specs = (
        P(ALL_AXES, None),
        P(SECTION_AXES, REP_AXES, None),
        P(SECTION_AXES, REP_AXES),
        P(SECTION_AXES, REP_AXES, None, None, None),
        P(),
        P(),
        P(ALL_AXES, None),
    )
    out_specs = (P(ALL_AXES, None), P(), P())
    return jax.shard_map(shards, mesh=fine, in_specs=in_specs, out_specs=out_specs, check_vma=False)
```

```python
import math

import jax
import jax.numpy as jnp
from jax import lax
from jax.experimental import pallas as pl
from jax.experimental.pallas import tpu as pltpu
from jax.sharding import Mesh
from jax.sharding import PartitionSpec as P

SECTION_AXES = ("y_hi", "z", "x")
REP_AXES = ("y_lo", "core")
ALL_AXES = SECTION_AXES + REP_AXES


def _xor_perm(n, bit):
    return [(i, i ^ bit) for i in range(n)]


def _halving_scatter(blocks, axis, n, bits):
    me = lax.axis_index(axis)
    depth = n.bit_length() - 1
    rest = blocks.shape[1:]
    blocks = blocks.reshape((2,) * depth + rest)
    left = list(range(depth - 1, -1, -1))
    for bit in bits:
        at = left.index(bit)
        mine = (me // (1 << bit)) % 2
        keep = lax.dynamic_index_in_dim(blocks, mine, at, keepdims=False)
        send = lax.dynamic_index_in_dim(blocks, 1 - mine, at, keepdims=False)
        blocks = keep + lax.ppermute(send, axis, _xor_perm(n, 1 << bit))
        left.pop(at)
    return blocks


def _doubling_gather(piece, axis, n, bits):
    me = lax.axis_index(axis)
    rest = piece.shape
    got = []
    for bit in bits:
        other = lax.ppermute(piece, axis, _xor_perm(n, 1 << bit))
        upper = (me // (1 << bit)) % 2 == 1
        low = jnp.where(upper, other, piece)
        high = jnp.where(upper, piece, other)
        piece = jnp.stack([low, high])
        got = [bit] + got
    order = sorted(range(len(got)), key=lambda i: -got[i])
    piece = jnp.transpose(piece, order + list(range(len(got), piece.ndim)))
    return piece.reshape((n * rest[0],) + rest[1:])


def _doubling_sum(piece, axis, n):
    bit = 1
    while bit < n:
        piece = piece + lax.ppermute(piece, axis, _xor_perm(n, bit))
        bit *= 2
    return piece


def _aggregate_kernel(cols_ref, tiles_ref, near_hbm, far_hbm, out_ref, buf, sems):
    groups, slots = out_ref.shape[0], buf.shape[1]
    half = near_hbm.shape[0]

    def start(g, slot):
        for k in range(slots):
            col = cols_ref[g * slots + k]

            @pl.when(col < half)
            def _near(col=col, k=k):
                pltpu.make_async_copy(near_hbm.at[col], buf.at[slot, k], sems.at[slot, k]).start()

            @pl.when(col >= half)
            def _far(col=col, k=k):
                pltpu.make_async_copy(far_hbm.at[col - half], buf.at[slot, k], sems.at[slot, k]).start()

    def wait(slot):
        for k in range(slots):
            pltpu.make_async_copy(near_hbm.at[0], buf.at[slot, k], sems.at[slot, k]).wait()

    start(0, 0)
    for g in range(groups):
        slot = g % 2
        if g + 1 < groups:
            start(g + 1, 1 - slot)
        wait(slot)
        rhs = buf[slot].reshape(slots * buf.shape[2], buf.shape[3])
        out_ref[g] = jnp.dot(tiles_ref[g], rhs, preferred_element_type=jnp.float32)


def _aggregate(cols, counts, tiles, near, far):
    groups, slots, tile_size, _ = tiles.shape
    feat_width = near.shape[-1]
    live = jnp.arange(slots, dtype=jnp.int32)[None, :] < counts[:, None]
    wide = jnp.where(live[:, :, None, None], tiles, jnp.zeros((), tiles.dtype))
    wide = wide.transpose(0, 2, 1, 3).reshape(groups, tile_size, slots * tile_size)
    flops = 2 * groups * slots * tile_size * tile_size * feat_width
    moved = tiles.size * 2 + groups * slots * tile_size * feat_width * 2 + groups * tile_size * feat_width * 4
    return pl.pallas_call(
        _aggregate_kernel,
        out_shape=jax.ShapeDtypeStruct((groups, tile_size, feat_width), jnp.float32),
        in_specs=[
            pl.BlockSpec(memory_space=pltpu.SMEM),
            pl.BlockSpec(memory_space=pltpu.VMEM),
            pl.BlockSpec(memory_space=pl.ANY),
            pl.BlockSpec(memory_space=pl.ANY),
        ],
        out_specs=pl.BlockSpec(memory_space=pltpu.VMEM),
        scratch_shapes=[
            pltpu.VMEM((2, slots, tile_size, feat_width), near.dtype),
            pltpu.SemaphoreType.DMA((2, slots)),
        ],
        cost_estimate=pl.CostEstimate(flops=flops, bytes_accessed=moved, transcendentals=0),
    )(jnp.clip(cols, 0, 2 * near.shape[0] - 1).reshape(-1), wide, near, far)


def shards(features, col_panels, block_counts, block_values, weight, bias, cotangent):
    sizes = {name: lax.axis_size(name) for name in ALL_AXES}
    rep_count = sizes["y_lo"] * sizes["core"]
    tile_size = block_values.shape[-1]
    feat_width = features.shape[1]
    own_panels = features.shape[0] // tile_size
    row_panels = col_panels.shape[0]
    global_cols = col_panels[:, 0, :]
    section_of = global_cols // (own_panels * rep_count)
    low = sizes["z"] * sizes["x"]
    far_side = (section_of // low != lax.axis_index("y_hi")).astype(jnp.int32)
    local_cols = (far_side * low + section_of % low) * own_panels + global_cols % own_panels
    live_counts = block_counts[:, 0]
    tiles = block_values[:, 0]
    near = lax.all_gather(features, ("z", "x"), axis=0, tiled=True)
    partner = lax.ppermute(features, "y_hi", _xor_perm(sizes["y_hi"], 1))
    far = lax.all_gather(partner, ("z", "x"), axis=0, tiled=True)
    near = near.reshape(-1, tile_size, feat_width)
    far = far.reshape(-1, tile_size, feat_width)
    gathered_sum = _aggregate(local_cols, live_counts, tiles, near, far)
    cores = sizes["core"]
    by_core = gathered_sum.reshape(row_panels // cores, cores, tile_size, feat_width)
    by_core = jnp.moveaxis(by_core, 1, 0)
    half = _halving_scatter(by_core, "core", cores, (0,))
    summed_own = _halving_scatter(half, "y_lo", sizes["y_lo"], (0, 1))
    own_rows = own_panels * tile_size
    aggregated = summed_own.reshape(own_rows, feat_width).astype(jnp.bfloat16)
    pre = jnp.dot(aggregated, weight, preferred_element_type=jnp.float32) + bias
    hidden = jax.nn.silu(pre).astype(jnp.bfloat16)
    sigmoid_pre = jax.nn.sigmoid(pre)
    slope = (
        cotangent.astype(jnp.float32) * (sigmoid_pre * (1.0 + pre * (1.0 - sigmoid_pre)))
    ).astype(jnp.bfloat16)
    local_weight = jnp.einsum("nd,nf->df", aggregated, slope, preferred_element_type=jnp.float32)
    local_bias = jnp.sum(slope.astype(jnp.float32), axis=0)
    width = weight.shape[0]
    scatter_ways = sizes["core"] * sizes["x"]
    padded_rows = -(-(width + 1) // (scatter_ways * 8)) * scatter_ways * 8
    combined = jnp.zeros((padded_rows, feat_width), jnp.float32)
    combined = combined.at[:width].set(local_weight).at[width].set(local_bias)
    chunk = _halving_scatter(combined.reshape(sizes["core"], -1, feat_width), "core", sizes["core"], (0,))
    chunk = _halving_scatter(chunk.reshape(sizes["x"], -1, feat_width), "x", sizes["x"], (0, 1))
    for name in ("y_lo", "z", "y_hi"):
        chunk = _doubling_sum(chunk, name, sizes[name])
    chunk = _doubling_gather(chunk, "x", sizes["x"], (1, 0))
    chunk = _doubling_gather(chunk, "core", sizes["core"], (0,))
    node_total = lax.axis_size(SECTION_AXES) * rep_count * own_rows
    factor = 1.0 / math.sqrt(node_total)
    weight_sum = chunk[:width]
    bias_sum = chunk[width]
    return (hidden, weight_sum * factor, bias_sum * factor)


def solution(mesh):
    section_size, rep_size = mesh.devices.shape
    fine = Mesh(mesh.devices.reshape(2, section_size // 8, 4, rep_size // 2, 2), ALL_AXES)
    in_specs = (
        P(ALL_AXES, None),
        P(SECTION_AXES, REP_AXES, None),
        P(SECTION_AXES, REP_AXES),
        P(SECTION_AXES, REP_AXES, None, None, None),
        P(),
        P(),
        P(ALL_AXES, None),
    )
    out_specs = (P(ALL_AXES, None), P(), P())
    return jax.shard_map(shards, mesh=fine, in_specs=in_specs, out_specs=out_specs, check_vma=False)
```

```python
import math

import jax
import jax.numpy as jnp
from jax import lax
from jax.experimental import pallas as pl
from jax.experimental.pallas import tpu as pltpu
from jax.sharding import Mesh
from jax.sharding import PartitionSpec as P

SECTION_AXES = ("y_hi", "z", "x")
REP_AXES = ("y_lo", "core")
ALL_AXES = SECTION_AXES + REP_AXES


def _xor_perm(n, bit):
    return [(i, i ^ bit) for i in range(n)]


def _halving_scatter(blocks, axis, n, bits):
    me = lax.axis_index(axis)
    depth = n.bit_length() - 1
    rest = blocks.shape[1:]
    blocks = blocks.reshape((2,) * depth + rest)
    left = list(range(depth - 1, -1, -1))
    for bit in bits:
        at = left.index(bit)
        mine = (me // (1 << bit)) % 2
        keep = lax.dynamic_index_in_dim(blocks, mine, at, keepdims=False)
        send = lax.dynamic_index_in_dim(blocks, 1 - mine, at, keepdims=False)
        blocks = keep + lax.ppermute(send, axis, _xor_perm(n, 1 << bit))
        left.pop(at)
    return blocks


def _doubling_gather(piece, axis, n, bits):
    me = lax.axis_index(axis)
    rest = piece.shape
    got = []
    for bit in bits:
        other = lax.ppermute(piece, axis, _xor_perm(n, 1 << bit))
        upper = (me // (1 << bit)) % 2 == 1
        low = jnp.where(upper, other, piece)
        high = jnp.where(upper, piece, other)
        piece = jnp.stack([low, high])
        got = [bit] + got
    order = sorted(range(len(got)), key=lambda i: -got[i])
    piece = jnp.transpose(piece, order + list(range(len(got), piece.ndim)))
    return piece.reshape((n * rest[0],) + rest[1:])


def _doubling_sum(piece, axis, n):
    bit = 1
    while bit < n:
        piece = piece + lax.ppermute(piece, axis, _xor_perm(n, bit))
        bit *= 2
    return piece


def _aggregate_kernel(cols_ref, tiles_ref, panels_hbm, out_ref, buf, sems):
    groups, slots = out_ref.shape[0], buf.shape[1]

    def copies(g, slot):
        return [
            pltpu.make_async_copy(panels_hbm.at[cols_ref[g * slots + k]], buf.at[slot, k], sems.at[slot, k])
            for k in range(slots)
        ]

    pending = copies(0, 0)
    for c in pending:
        c.start()
    for g in range(groups):
        slot = g % 2
        if g + 1 < groups:
            ahead = copies(g + 1, 1 - slot)
            for c in ahead:
                c.start()
        for c in pending:
            c.wait()
        rhs = buf[slot].reshape(slots * buf.shape[2], buf.shape[3])
        out_ref[g] = jnp.dot(tiles_ref[g], rhs, preferred_element_type=jnp.float32)
        if g + 1 < groups:
            pending = ahead


def _aggregate(cols, counts, tiles, panels):
    groups, slots, tile_size, _ = tiles.shape
    feat_width = panels.shape[-1]
    live = jnp.arange(slots, dtype=jnp.int32)[None, :] < counts[:, None]
    wide = jnp.where(live[:, :, None, None], tiles, jnp.zeros((), tiles.dtype))
    wide = wide.transpose(0, 2, 1, 3).reshape(groups, tile_size, slots * tile_size)
    flops = 2 * groups * slots * tile_size * tile_size * feat_width
    moved = tiles.size * 2 + groups * slots * tile_size * feat_width * 2 + groups * tile_size * feat_width * 4
    return pl.pallas_call(
        _aggregate_kernel,
        out_shape=jax.ShapeDtypeStruct((groups, tile_size, feat_width), jnp.float32),
        in_specs=[
            pl.BlockSpec(memory_space=pltpu.SMEM),
            pl.BlockSpec(memory_space=pltpu.VMEM),
            pl.BlockSpec(memory_space=pltpu.VMEM),
        ],
        out_specs=pl.BlockSpec(memory_space=pltpu.VMEM),
        scratch_shapes=[
            pltpu.VMEM((2, slots, tile_size, feat_width), panels.dtype),
            pltpu.SemaphoreType.DMA((2, slots)),
        ],
        cost_estimate=pl.CostEstimate(flops=flops, bytes_accessed=moved, transcendentals=0),
    )(jnp.clip(cols, 0, panels.shape[0] - 1).reshape(-1), wide, panels)


def shards(features, col_panels, block_counts, block_values, weight, bias, cotangent):
    sizes = {name: lax.axis_size(name) for name in ALL_AXES}
    rep_count = sizes["y_lo"] * sizes["core"]
    tile_size = block_values.shape[-1]
    feat_width = features.shape[1]
    own_panels = features.shape[0] // tile_size
    row_panels = col_panels.shape[0]
    global_cols = col_panels[:, 0, :]
    section_of = global_cols // (own_panels * rep_count)
    low = sizes["z"] * sizes["x"]
    gathered_pos = (section_of % low) * sizes["y_hi"] + section_of // low
    local_cols = gathered_pos * own_panels + global_cols % own_panels
    live_counts = block_counts[:, 0]
    tiles = block_values[:, 0]
    gathered = lax.all_gather(features, "y_hi", axis=0, tiled=True)
    gathered = lax.all_gather(gathered, ("z", "x"), axis=0, tiled=True)
    all_panels = gathered.reshape(-1, tile_size, feat_width)
    gathered_sum = _aggregate(local_cols, live_counts, tiles, all_panels)
    cores = sizes["core"]
    by_core = gathered_sum.reshape(row_panels // cores, cores, tile_size, feat_width)
    by_core = jnp.moveaxis(by_core, 1, 0)
    half = _halving_scatter(by_core, "core", cores, (0,))
    summed_own = _halving_scatter(half, "y_lo", sizes["y_lo"], (0, 1))
    own_rows = own_panels * tile_size
    aggregated = summed_own.reshape(own_rows, feat_width).astype(jnp.bfloat16)
    pre = jnp.dot(aggregated, weight, preferred_element_type=jnp.float32) + bias
    hidden = jax.nn.silu(pre).astype(jnp.bfloat16)
    sigmoid_pre = jax.nn.sigmoid(pre)
    slope = (
        cotangent.astype(jnp.float32) * (sigmoid_pre * (1.0 + pre * (1.0 - sigmoid_pre)))
    ).astype(jnp.bfloat16)
    local_weight = jnp.einsum("nd,nf->df", aggregated, slope, preferred_element_type=jnp.float32)
    local_bias = jnp.sum(slope.astype(jnp.float32), axis=0)
    width = weight.shape[0]
    scatter_ways = sizes["core"] * sizes["x"]
    padded_rows = -(-(width + 1) // (scatter_ways * 8)) * scatter_ways * 8
    combined = jnp.zeros((padded_rows, feat_width), jnp.float32)
    combined = combined.at[:width].set(local_weight).at[width].set(local_bias)
    chunk = _halving_scatter(combined.reshape(sizes["core"], -1, feat_width), "core", sizes["core"], (0,))
    chunk = _halving_scatter(chunk.reshape(sizes["x"], -1, feat_width), "x", sizes["x"], (0, 1))
    for name in ("y_lo", "z", "y_hi"):
        chunk = _doubling_sum(chunk, name, sizes[name])
    chunk = _doubling_gather(chunk, "x", sizes["x"], (1, 0))
    chunk = _doubling_gather(chunk, "core", sizes["core"], (0,))
    node_total = lax.axis_size(SECTION_AXES) * rep_count * own_rows
    factor = 1.0 / math.sqrt(node_total)
    weight_sum = chunk[:width]
    bias_sum = chunk[width]
    return (hidden, weight_sum * factor, bias_sum * factor)


def solution(mesh):
    section_size, rep_size = mesh.devices.shape
    fine = Mesh(mesh.devices.reshape(2, section_size // 8, 4, rep_size // 2, 2), ALL_AXES)
    in_specs = (
        P(ALL_AXES, None),
        P(SECTION_AXES, REP_AXES, None),
        P(SECTION_AXES, REP_AXES),
        P(SECTION_AXES, REP_AXES, None, None, None),
        P(),
        P(),
        P(ALL_AXES, None),
    )
    out_specs = (P(ALL_AXES, None), P(), P())
    return jax.shard_map(shards, mesh=fine, in_specs=in_specs, out_specs=out_specs, check_vma=False)
```

```python
import math

import jax
import jax.numpy as jnp
from jax import lax
from jax.experimental import pallas as pl
from jax.experimental.pallas import tpu as pltpu
from jax.sharding import Mesh
from jax.sharding import PartitionSpec as P

SECTION_AXES = ("y_hi", "z", "x")
REP_AXES = ("y_lo", "core")
ALL_AXES = SECTION_AXES + REP_AXES


def _xor_perm(n, bit):
    return [(i, i ^ bit) for i in range(n)]


def _halving_scatter(blocks, axis, n, bits):
    me = lax.axis_index(axis)
    depth = n.bit_length() - 1
    rest = blocks.shape[1:]
    blocks = blocks.reshape((2,) * depth + rest)
    left = list(range(depth - 1, -1, -1))
    for bit in bits:
        at = left.index(bit)
        mine = (me // (1 << bit)) % 2
        keep = lax.dynamic_index_in_dim(blocks, mine, at, keepdims=False)
        send = lax.dynamic_index_in_dim(blocks, 1 - mine, at, keepdims=False)
        blocks = keep + lax.ppermute(send, axis, _xor_perm(n, 1 << bit))
        left.pop(at)
    return blocks


def _doubling_gather(piece, axis, n, bits):
    me = lax.axis_index(axis)
    rest = piece.shape
    got = []
    for bit in bits:
        other = lax.ppermute(piece, axis, _xor_perm(n, 1 << bit))
        upper = (me // (1 << bit)) % 2 == 1
        low = jnp.where(upper, other, piece)
        high = jnp.where(upper, piece, other)
        piece = jnp.stack([low, high])
        got = [bit] + got
    order = sorted(range(len(got)), key=lambda i: -got[i])
    piece = jnp.transpose(piece, order + list(range(len(got), piece.ndim)))
    return piece.reshape((n * rest[0],) + rest[1:])


def _doubling_sum(piece, axis, n):
    bit = 1
    while bit < n:
        piece = piece + lax.ppermute(piece, axis, _xor_perm(n, bit))
        bit *= 2
    return piece


def _aggregate_kernel(cols_ref, tiles_ref, panels_hbm, out_ref, buf, sems):
    groups, slots = out_ref.shape[0], buf.shape[1]

    def copies(g, slot):
        return [
            pltpu.make_async_copy(panels_hbm.at[cols_ref[g * slots + k]], buf.at[slot, k], sems.at[slot, k])
            for k in range(slots)
        ]

    pending = copies(0, 0)
    for c in pending:
        c.start()
    for g in range(groups):
        slot = g % 2
        if g + 1 < groups:
            ahead = copies(g + 1, 1 - slot)
            for c in ahead:
                c.start()
        for c in pending:
            c.wait()
        rhs = buf[slot].reshape(slots * buf.shape[2], buf.shape[3])
        out_ref[g] = jnp.dot(tiles_ref[g], rhs, preferred_element_type=jnp.float32)
        if g + 1 < groups:
            pending = ahead


def _aggregate(cols, counts, tiles, panels):
    groups, slots, tile_size, _ = tiles.shape
    feat_width = panels.shape[-1]
    live = jnp.arange(slots, dtype=jnp.int32)[None, :] < counts[:, None]
    wide = jnp.where(live[:, :, None, None], tiles, jnp.zeros((), tiles.dtype))
    wide = wide.transpose(0, 2, 1, 3).reshape(groups, tile_size, slots * tile_size)
    flops = 2 * groups * slots * tile_size * tile_size * feat_width
    moved = tiles.size * 2 + groups * slots * tile_size * feat_width * 2 + groups * tile_size * feat_width * 4
    return pl.pallas_call(
        _aggregate_kernel,
        out_shape=jax.ShapeDtypeStruct((groups, tile_size, feat_width), jnp.float32),
        in_specs=[
            pl.BlockSpec(memory_space=pltpu.SMEM),
            pl.BlockSpec(memory_space=pltpu.VMEM),
            pl.BlockSpec(memory_space=pl.ANY),
        ],
        out_specs=pl.BlockSpec(memory_space=pltpu.VMEM),
        scratch_shapes=[
            pltpu.VMEM((2, slots, tile_size, feat_width), panels.dtype),
            pltpu.SemaphoreType.DMA((2, slots)),
        ],
        cost_estimate=pl.CostEstimate(flops=flops, bytes_accessed=moved, transcendentals=0),
    )(jnp.clip(cols, 0, panels.shape[0] - 1).reshape(-1), wide, panels)


def shards(features, col_panels, block_counts, block_values, weight, bias, cotangent):
    sizes = {name: lax.axis_size(name) for name in ALL_AXES}
    rep_count = sizes["y_lo"] * sizes["core"]
    tile_size = block_values.shape[-1]
    feat_width = features.shape[1]
    own_panels = features.shape[0] // tile_size
    row_panels = col_panels.shape[0]
    global_cols = col_panels[:, 0, :]
    section_of = global_cols // (own_panels * rep_count)
    low = sizes["z"] * sizes["x"]
    gathered_pos = (section_of % low) * sizes["y_hi"] + section_of // low
    local_cols = gathered_pos * own_panels + global_cols % own_panels
    live_counts = block_counts[:, 0]
    tiles = block_values[:, 0]
    gathered = lax.all_gather(features, "y_hi", axis=0, tiled=True)
    gathered = lax.all_gather(gathered, ("z", "x"), axis=0, tiled=True)
    all_panels = gathered.reshape(-1, tile_size, feat_width)
    cores = sizes["core"]
    me_core = lax.axis_index("core")
    split = lambda a: a.reshape((row_panels // cores, cores) + a.shape[1:])
    pick = lambda a, c: lax.dynamic_index_in_dim(split(a), c, 1, keepdims=False)
    other = 1 - me_core
    sent = _aggregate(pick(local_cols, other), pick(live_counts, other), pick(tiles, other), all_panels)
    arrived = lax.ppermute(sent, "core", _xor_perm(cores, 1))
    kept = _aggregate(pick(local_cols, me_core), pick(live_counts, me_core), pick(tiles, me_core), all_panels)
    half = kept + arrived
    summed_own = _halving_scatter(half, "y_lo", sizes["y_lo"], (0, 1))
    own_rows = own_panels * tile_size
    aggregated = summed_own.reshape(own_rows, feat_width).astype(jnp.bfloat16)
    pre = jnp.dot(aggregated, weight, preferred_element_type=jnp.float32) + bias
    hidden = jax.nn.silu(pre).astype(jnp.bfloat16)
    sigmoid_pre = jax.nn.sigmoid(pre)
    slope = (
        cotangent.astype(jnp.float32) * (sigmoid_pre * (1.0 + pre * (1.0 - sigmoid_pre)))
    ).astype(jnp.bfloat16)
    local_weight = jnp.einsum("nd,nf->df", aggregated, slope, preferred_element_type=jnp.float32)
    local_bias = jnp.sum(slope.astype(jnp.float32), axis=0)
    width = weight.shape[0]
    scatter_ways = sizes["core"] * sizes["x"]
    padded_rows = -(-(width + 1) // (scatter_ways * 8)) * scatter_ways * 8
    combined = jnp.zeros((padded_rows, feat_width), jnp.float32)
    combined = combined.at[:width].set(local_weight).at[width].set(local_bias)
    chunk = _halving_scatter(combined.reshape(sizes["core"], -1, feat_width), "core", sizes["core"], (0,))
    chunk = _halving_scatter(chunk.reshape(sizes["x"], -1, feat_width), "x", sizes["x"], (0, 1))
    for name in ("y_lo", "z", "y_hi"):
        chunk = _doubling_sum(chunk, name, sizes[name])
    chunk = _doubling_gather(chunk, "x", sizes["x"], (1, 0))
    chunk = _doubling_gather(chunk, "core", sizes["core"], (0,))
    node_total = lax.axis_size(SECTION_AXES) * rep_count * own_rows
    factor = 1.0 / math.sqrt(node_total)
    weight_sum = chunk[:width]
    bias_sum = chunk[width]
    return (hidden, weight_sum * factor, bias_sum * factor)


def solution(mesh):
    section_size, rep_size = mesh.devices.shape
    fine = Mesh(mesh.devices.reshape(2, section_size // 8, 4, rep_size // 2, 2), ALL_AXES)
    in_specs = (
        P(ALL_AXES, None),
        P(SECTION_AXES, REP_AXES, None),
        P(SECTION_AXES, REP_AXES),
        P(SECTION_AXES, REP_AXES, None, None, None),
        P(),
        P(),
        P(ALL_AXES, None),
    )
    out_specs = (P(ALL_AXES, None), P(), P())
    return jax.shard_map(shards, mesh=fine, in_specs=in_specs, out_specs=out_specs, check_vma=False)
```

```python
import math

import jax
import jax.numpy as jnp
from jax import lax
from jax.experimental import pallas as pl
from jax.experimental.pallas import tpu as pltpu
from jax.sharding import Mesh
from jax.sharding import PartitionSpec as P

SECTION_AXES = ("y_hi", "z", "x")
REP_AXES = ("y_lo", "core")
ALL_AXES = SECTION_AXES + REP_AXES


def _xor_perm(n, bit):
    return [(i, i ^ bit) for i in range(n)]


def _halving_scatter(blocks, axis, n, bits):
    me = lax.axis_index(axis)
    depth = n.bit_length() - 1
    rest = blocks.shape[1:]
    blocks = blocks.reshape((2,) * depth + rest)
    left = list(range(depth - 1, -1, -1))
    for bit in bits:
        at = left.index(bit)
        mine = (me // (1 << bit)) % 2
        keep = lax.dynamic_index_in_dim(blocks, mine, at, keepdims=False)
        send = lax.dynamic_index_in_dim(blocks, 1 - mine, at, keepdims=False)
        blocks = keep + lax.ppermute(send, axis, _xor_perm(n, 1 << bit))
        left.pop(at)
    return blocks


def _doubling_gather(piece, axis, n, bits):
    me = lax.axis_index(axis)
    rest = piece.shape
    got = []
    for bit in bits:
        other = lax.ppermute(piece, axis, _xor_perm(n, 1 << bit))
        upper = (me // (1 << bit)) % 2 == 1
        low = jnp.where(upper, other, piece)
        high = jnp.where(upper, piece, other)
        piece = jnp.stack([low, high])
        got = [bit] + got
    order = sorted(range(len(got)), key=lambda i: -got[i])
    piece = jnp.transpose(piece, order + list(range(len(got), piece.ndim)))
    return piece.reshape((n * rest[0],) + rest[1:])


def _doubling_sum(piece, axis, n):
    bit = 1
    while bit < n:
        piece = piece + lax.ppermute(piece, axis, _xor_perm(n, bit))
        bit *= 2
    return piece


def _aggregate_kernel(parity_ref, cols_ref, tiles_ref, panels_hbm, out_ref, buf, sems):
    groups, slots = out_ref.shape[0], buf.shape[1]
    stride = tiles_ref.shape[0] // groups
    parity = parity_ref[0]

    def copies(j, slot):
        g = stride * j + parity
        return [
            pltpu.make_async_copy(panels_hbm.at[cols_ref[g * slots + k]], buf.at[slot, k], sems.at[slot, k])
            for k in range(slots)
        ]

    pending = copies(0, 0)
    for c in pending:
        c.start()
    for j in range(groups):
        slot = j % 2
        if j + 1 < groups:
            ahead = copies(j + 1, 1 - slot)
            for c in ahead:
                c.start()
        for c in pending:
            c.wait()
        rhs = buf[slot].reshape(slots * buf.shape[2], buf.shape[3])
        out_ref[j] = jnp.dot(tiles_ref[stride * j + parity], rhs, preferred_element_type=jnp.float32)
        if j + 1 < groups:
            pending = ahead


def _widen(counts, tiles):
    groups, slots, tile_size, _ = tiles.shape
    live = jnp.arange(slots, dtype=jnp.int32)[None, :] < counts[:, None]
    wide = jnp.where(live[:, :, None, None], tiles, jnp.zeros((), tiles.dtype))
    return wide.transpose(0, 2, 1, 3).reshape(groups, tile_size, slots * tile_size)


def _aggregate(cols, wide, panels, parity, stride):
    groups, tile_size, width = wide.shape
    slots = width // tile_size
    feat_width = panels.shape[-1]
    picked = groups // stride
    flops = 2 * picked * slots * tile_size * tile_size * feat_width
    moved = (picked * tile_size * width * 2 + picked * slots * tile_size * feat_width * 2
             + picked * tile_size * feat_width * 4)
    return pl.pallas_call(
        _aggregate_kernel,
        out_shape=jax.ShapeDtypeStruct((picked, tile_size, feat_width), jnp.float32),
        in_specs=[
            pl.BlockSpec(memory_space=pltpu.SMEM),
            pl.BlockSpec(memory_space=pltpu.SMEM),
            pl.BlockSpec(memory_space=pltpu.VMEM),
            pl.BlockSpec(memory_space=pl.ANY),
        ],
        out_specs=pl.BlockSpec(memory_space=pltpu.VMEM),
        scratch_shapes=[
            pltpu.VMEM((2, slots, tile_size, feat_width), panels.dtype),
            pltpu.SemaphoreType.DMA((2, slots)),
        ],
        cost_estimate=pl.CostEstimate(flops=flops, bytes_accessed=moved, transcendentals=0),
    )(jnp.reshape(parity, (1,)).astype(jnp.int32), cols, wide, panels)


def shards(features, col_panels, block_counts, block_values, weight, bias, cotangent):
    sizes = {name: lax.axis_size(name) for name in ALL_AXES}
    rep_count = sizes["y_lo"] * sizes["core"]
    tile_size = block_values.shape[-1]
    feat_width = features.shape[1]
    own_panels = features.shape[0] // tile_size
    row_panels = col_panels.shape[0]
    global_cols = col_panels[:, 0, :]
    section_of = global_cols // (own_panels * rep_count)
    low = sizes["z"] * sizes["x"]
    gathered_pos = (section_of % low) * sizes["y_hi"] + section_of // low
    local_cols = gathered_pos * own_panels + global_cols % own_panels
    live_counts = block_counts[:, 0]
    tiles = block_values[:, 0]
    gathered = lax.all_gather(features, "y_hi", axis=0, tiled=True)
    gathered = lax.all_gather(gathered, ("z", "x"), axis=0, tiled=True)
    all_panels = gathered.reshape(-1, tile_size, feat_width)
    wide = _widen(live_counts, tiles)
    cols = jnp.clip(local_cols, 0, all_panels.shape[0] - 1).reshape(-1)
    cores = sizes["core"]
    me_core = lax.axis_index("core")
    sent = _aggregate(cols, wide, all_panels, cores - 1 - me_core, cores)
    arrived = lax.ppermute(sent, "core", _xor_perm(cores, 1))
    kept = _aggregate(cols, wide, all_panels, me_core, cores)
    half = kept + arrived
    summed_own = _halving_scatter(half, "y_lo", sizes["y_lo"], (0, 1))
    own_rows = own_panels * tile_size
    aggregated = summed_own.reshape(own_rows, feat_width).astype(jnp.bfloat16)
    pre = jnp.dot(aggregated, weight, preferred_element_type=jnp.float32) + bias
    hidden = jax.nn.silu(pre).astype(jnp.bfloat16)
    sigmoid_pre = jax.nn.sigmoid(pre)
    slope = (
        cotangent.astype(jnp.float32) * (sigmoid_pre * (1.0 + pre * (1.0 - sigmoid_pre)))
    ).astype(jnp.bfloat16)
    local_weight = jnp.einsum("nd,nf->df", aggregated, slope, preferred_element_type=jnp.float32)
    local_bias = jnp.sum(slope.astype(jnp.float32), axis=0)
    width = weight.shape[0]
    scatter_ways = sizes["core"] * sizes["x"]
    padded_rows = -(-(width + 1) // (scatter_ways * 8)) * scatter_ways * 8
    combined = jnp.zeros((padded_rows, feat_width), jnp.float32)
    combined = combined.at[:width].set(local_weight).at[width].set(local_bias)
    chunk = _halving_scatter(combined.reshape(sizes["core"], -1, feat_width), "core", sizes["core"], (0,))
    chunk = _halving_scatter(chunk.reshape(sizes["x"], -1, feat_width), "x", sizes["x"], (0, 1))
    for name in ("y_lo", "z", "y_hi"):
        chunk = _doubling_sum(chunk, name, sizes[name])
    chunk = _doubling_gather(chunk, "x", sizes["x"], (1, 0))
    chunk = _doubling_gather(chunk, "core", sizes["core"], (0,))
    node_total = lax.axis_size(SECTION_AXES) * rep_count * own_rows
    factor = 1.0 / math.sqrt(node_total)
    weight_sum = chunk[:width]
    bias_sum = chunk[width]
    return (hidden, weight_sum * factor, bias_sum * factor)


def solution(mesh):
    section_size, rep_size = mesh.devices.shape
    fine = Mesh(mesh.devices.reshape(2, section_size // 8, 4, rep_size // 2, 2), ALL_AXES)
    in_specs = (
        P(ALL_AXES, None),
        P(SECTION_AXES, REP_AXES, None),
        P(SECTION_AXES, REP_AXES),
        P(SECTION_AXES, REP_AXES, None, None, None),
        P(),
        P(),
        P(ALL_AXES, None),
    )
    out_specs = (P(ALL_AXES, None), P(), P())
    return jax.shard_map(shards, mesh=fine, in_specs=in_specs, out_specs=out_specs, check_vma=False)
```

```python
import math

import jax
import jax.numpy as jnp
from jax import lax
from jax.experimental import pallas as pl
from jax.experimental.pallas import tpu as pltpu
from jax.sharding import Mesh
from jax.sharding import PartitionSpec as P

SECTION_AXES = ("y_hi", "z", "x")
REP_AXES = ("y_lo", "core")
ALL_AXES = SECTION_AXES + REP_AXES


def _xor_perm(n, bit):
    return [(i, i ^ bit) for i in range(n)]


def _halving_scatter(blocks, axis, n, bits):
    me = lax.axis_index(axis)
    depth = n.bit_length() - 1
    rest = blocks.shape[1:]
    blocks = blocks.reshape((2,) * depth + rest)
    left = list(range(depth - 1, -1, -1))
    for bit in bits:
        at = left.index(bit)
        mine = (me // (1 << bit)) % 2
        keep = lax.dynamic_index_in_dim(blocks, mine, at, keepdims=False)
        send = lax.dynamic_index_in_dim(blocks, 1 - mine, at, keepdims=False)
        blocks = keep + lax.ppermute(send, axis, _xor_perm(n, 1 << bit))
        left.pop(at)
    return blocks


def _doubling_gather(piece, axis, n, bits):
    me = lax.axis_index(axis)
    rest = piece.shape
    got = []
    for bit in bits:
        other = lax.ppermute(piece, axis, _xor_perm(n, 1 << bit))
        upper = (me // (1 << bit)) % 2 == 1
        low = jnp.where(upper, other, piece)
        high = jnp.where(upper, piece, other)
        piece = jnp.stack([low, high])
        got = [bit] + got
    order = sorted(range(len(got)), key=lambda i: -got[i])
    piece = jnp.transpose(piece, order + list(range(len(got), piece.ndim)))
    return piece.reshape((n * rest[0],) + rest[1:])


def _doubling_sum(piece, axis, n):
    bit = 1
    while bit < n:
        piece = piece + lax.ppermute(piece, axis, _xor_perm(n, bit))
        bit *= 2
    return piece


def _aggregate_kernel(rows_ref, cols_ref, tiles_ref, panels_hbm, out_ref, buf, sems):
    groups, slots = out_ref.shape[0], buf.shape[1]

    def copies(j, slot):
        g = rows_ref[j]
        return [
            pltpu.make_async_copy(panels_hbm.at[cols_ref[g * slots + k]], buf.at[slot, k], sems.at[slot, k])
            for k in range(slots)
        ]

    pending = copies(0, 0)
    for c in pending:
        c.start()
    for j in range(groups):
        slot = j % 2
        if j + 1 < groups:
            ahead = copies(j + 1, 1 - slot)
            for c in ahead:
                c.start()
        for c in pending:
            c.wait()
        rhs = buf[slot].reshape(slots * buf.shape[2], buf.shape[3])
        out_ref[j] = jnp.dot(tiles_ref[rows_ref[j]], rhs, preferred_element_type=jnp.float32)
        if j + 1 < groups:
            pending = ahead


def _widen(counts, tiles):
    groups, slots, tile_size, _ = tiles.shape
    live = jnp.arange(slots, dtype=jnp.int32)[None, :] < counts[:, None]
    wide = jnp.where(live[:, :, None, None], tiles, jnp.zeros((), tiles.dtype))
    return wide.transpose(0, 2, 1, 3).reshape(groups, tile_size, slots * tile_size)


def _aggregate(cols, wide, panels, rows):
    groups, tile_size, width = wide.shape
    slots = width // tile_size
    feat_width = panels.shape[-1]
    picked = rows.shape[0]
    flops = 2 * picked * slots * tile_size * tile_size * feat_width
    moved = (picked * tile_size * width * 2 + picked * slots * tile_size * feat_width * 2
             + picked * tile_size * feat_width * 4)
    return pl.pallas_call(
        _aggregate_kernel,
        out_shape=jax.ShapeDtypeStruct((picked, tile_size, feat_width), jnp.float32),
        in_specs=[
            pl.BlockSpec(memory_space=pltpu.SMEM),
            pl.BlockSpec(memory_space=pltpu.SMEM),
            pl.BlockSpec(memory_space=pltpu.VMEM),
            pl.BlockSpec(memory_space=pl.ANY),
        ],
        out_specs=pl.BlockSpec(memory_space=pltpu.VMEM),
        scratch_shapes=[
            pltpu.VMEM((2, slots, tile_size, feat_width), panels.dtype),
            pltpu.SemaphoreType.DMA((2, slots)),
        ],
        cost_estimate=pl.CostEstimate(flops=flops, bytes_accessed=moved, transcendentals=0),
    )(jnp.clip(rows, 0, groups - 1).astype(jnp.int32), cols, wide, panels)


def shards(features, col_panels, block_counts, block_values, weight, bias, cotangent):
    sizes = {name: lax.axis_size(name) for name in ALL_AXES}
    rep_count = sizes["y_lo"] * sizes["core"]
    tile_size = block_values.shape[-1]
    feat_width = features.shape[1]
    own_panels = features.shape[0] // tile_size
    row_panels = col_panels.shape[0]
    global_cols = col_panels[:, 0, :]
    section_of = global_cols // (own_panels * rep_count)
    low = sizes["z"] * sizes["x"]
    gathered_pos = (section_of % low) * sizes["y_hi"] + section_of // low
    local_cols = gathered_pos * own_panels + global_cols % own_panels
    live_counts = block_counts[:, 0]
    tiles = block_values[:, 0]
    gathered = lax.all_gather(features, "y_hi", axis=0, tiled=True)
    gathered = lax.all_gather(gathered, ("z", "x"), axis=0, tiled=True)
    all_panels = gathered.reshape(-1, tile_size, feat_width)
    wide = _widen(live_counts, tiles)
    cols = jnp.clip(local_cols, 0, all_panels.shape[0] - 1).reshape(-1)
    cores = sizes["core"]
    me_core = lax.axis_index("core")
    me_y = lax.axis_index("y_lo")
    low_bit, high_bit = me_y % 2, (me_y // 2) % 2
    j = jnp.arange(4, dtype=jnp.int32)
    ys = ((high_bit ^ (j % 2)) * 2 + (low_bit ^ (j // 2))).astype(jnp.int32)
    sent = _aggregate(cols, wide, all_panels, ys * cores + (cores - 1 - me_core))
    arrived = lax.ppermute(sent, "core", _xor_perm(cores, 1))
    kept = _aggregate(cols, wide, all_panels, ys * cores + me_core)
    half = kept + arrived
    after = half[:2] + lax.ppermute(half[2:], "y_lo", _xor_perm(sizes["y_lo"], 1))
    summed_own = after[0] + lax.ppermute(after[1], "y_lo", _xor_perm(sizes["y_lo"], 2))
    own_rows = own_panels * tile_size
    aggregated = summed_own.reshape(own_rows, feat_width).astype(jnp.bfloat16)
    pre = jnp.dot(aggregated, weight, preferred_element_type=jnp.float32) + bias
    hidden = jax.nn.silu(pre).astype(jnp.bfloat16)
    sigmoid_pre = jax.nn.sigmoid(pre)
    slope = (
        cotangent.astype(jnp.float32) * (sigmoid_pre * (1.0 + pre * (1.0 - sigmoid_pre)))
    ).astype(jnp.bfloat16)
    local_weight = jnp.einsum("nd,nf->df", aggregated, slope, preferred_element_type=jnp.float32)
    local_bias = jnp.sum(slope.astype(jnp.float32), axis=0)
    width = weight.shape[0]
    scatter_ways = sizes["core"] * sizes["x"]
    padded_rows = -(-(width + 1) // (scatter_ways * 8)) * scatter_ways * 8
    combined = jnp.zeros((padded_rows, feat_width), jnp.float32)
    combined = combined.at[:width].set(local_weight).at[width].set(local_bias)
    chunk = _halving_scatter(combined.reshape(sizes["core"], -1, feat_width), "core", sizes["core"], (0,))
    chunk = _halving_scatter(chunk.reshape(sizes["x"], -1, feat_width), "x", sizes["x"], (0, 1))
    for name in ("y_lo", "z", "y_hi"):
        chunk = _doubling_sum(chunk, name, sizes[name])
    chunk = _doubling_gather(chunk, "x", sizes["x"], (1, 0))
    chunk = _doubling_gather(chunk, "core", sizes["core"], (0,))
    node_total = lax.axis_size(SECTION_AXES) * rep_count * own_rows
    factor = 1.0 / math.sqrt(node_total)
    weight_sum = chunk[:width]
    bias_sum = chunk[width]
    return (hidden, weight_sum * factor, bias_sum * factor)


def solution(mesh):
    section_size, rep_size = mesh.devices.shape
    fine = Mesh(mesh.devices.reshape(2, section_size // 8, 4, rep_size // 2, 2), ALL_AXES)
    in_specs = (
        P(ALL_AXES, None),
        P(SECTION_AXES, REP_AXES, None),
        P(SECTION_AXES, REP_AXES),
        P(SECTION_AXES, REP_AXES, None, None, None),
        P(),
        P(),
        P(ALL_AXES, None),
    )
    out_specs = (P(ALL_AXES, None), P(), P())
    return jax.shard_map(shards, mesh=fine, in_specs=in_specs, out_specs=out_specs, check_vma=False)
```

```python
import math

import jax
import jax.numpy as jnp
from jax import lax
from jax.experimental import pallas as pl
from jax.experimental.pallas import tpu as pltpu
from jax.sharding import Mesh
from jax.sharding import PartitionSpec as P

SECTION_AXES = ("y_hi", "z", "x")
REP_AXES = ("y_lo", "core")
ALL_AXES = SECTION_AXES + REP_AXES


def _xor_perm(n, bit):
    return [(i, i ^ bit) for i in range(n)]


def _halving_scatter(blocks, axis, n, bits):
    me = lax.axis_index(axis)
    depth = n.bit_length() - 1
    rest = blocks.shape[1:]
    blocks = blocks.reshape((2,) * depth + rest)
    left = list(range(depth - 1, -1, -1))
    for bit in bits:
        at = left.index(bit)
        mine = (me // (1 << bit)) % 2
        keep = lax.dynamic_index_in_dim(blocks, mine, at, keepdims=False)
        send = lax.dynamic_index_in_dim(blocks, 1 - mine, at, keepdims=False)
        blocks = keep + lax.ppermute(send, axis, _xor_perm(n, 1 << bit))
        left.pop(at)
    return blocks


def _doubling_gather(piece, axis, n, bits):
    me = lax.axis_index(axis)
    rest = piece.shape
    got = []
    for bit in bits:
        other = lax.ppermute(piece, axis, _xor_perm(n, 1 << bit))
        upper = (me // (1 << bit)) % 2 == 1
        low = jnp.where(upper, other, piece)
        high = jnp.where(upper, piece, other)
        piece = jnp.stack([low, high])
        got = [bit] + got
    order = sorted(range(len(got)), key=lambda i: -got[i])
    piece = jnp.transpose(piece, order + list(range(len(got), piece.ndim)))
    return piece.reshape((n * rest[0],) + rest[1:])


def _doubling_sum(piece, axis, n):
    bit = 1
    while bit < n:
        piece = piece + lax.ppermute(piece, axis, _xor_perm(n, bit))
        bit *= 2
    return piece


def _aggregate_kernel(parity_ref, cols_ref, tiles_ref, panels_hbm, out_ref, buf, sems, tbuf, tsems):
    groups, slots = out_ref.shape[0], buf.shape[1]
    stride = tiles_ref.shape[0] // groups
    parity = parity_ref[0]

    def copies(j, slot):
        g = stride * j + parity
        return [
            pltpu.make_async_copy(panels_hbm.at[cols_ref[g * slots + k]], buf.at[slot, k], sems.at[slot, k])
            for k in range(slots)
        ] + [pltpu.make_async_copy(tiles_ref.at[g], tbuf.at[slot], tsems.at[slot])]

    pending = copies(0, 0)
    for c in pending:
        c.start()
    for j in range(groups):
        slot = j % 2
        if j + 1 < groups:
            ahead = copies(j + 1, 1 - slot)
            for c in ahead:
                c.start()
        for c in pending:
            c.wait()
        rhs = buf[slot].reshape(slots * buf.shape[2], buf.shape[3])
        out_ref[j] = jnp.dot(tbuf[slot], rhs, preferred_element_type=jnp.float32)
        if j + 1 < groups:
            pending = ahead


def _widen(counts, tiles):
    groups, slots, tile_size, _ = tiles.shape
    live = jnp.arange(slots, dtype=jnp.int32)[None, :] < counts[:, None]
    wide = jnp.where(live[:, :, None, None], tiles, jnp.zeros((), tiles.dtype))
    return wide.transpose(0, 2, 1, 3).reshape(groups, tile_size, slots * tile_size)


def _aggregate(cols, wide, panels, parity, stride):
    groups, tile_size, width = wide.shape
    slots = width // tile_size
    feat_width = panels.shape[-1]
    picked = groups // stride
    flops = 2 * picked * slots * tile_size * tile_size * feat_width
    moved = (picked * tile_size * width * 2 + picked * slots * tile_size * feat_width * 2
             + picked * tile_size * feat_width * 4)
    return pl.pallas_call(
        _aggregate_kernel,
        out_shape=jax.ShapeDtypeStruct((picked, tile_size, feat_width), jnp.float32),
        in_specs=[
            pl.BlockSpec(memory_space=pltpu.SMEM),
            pl.BlockSpec(memory_space=pltpu.SMEM),
            pl.BlockSpec(memory_space=pl.ANY),
            pl.BlockSpec(memory_space=pl.ANY),
        ],
        out_specs=pl.BlockSpec(memory_space=pltpu.VMEM),
        scratch_shapes=[
            pltpu.VMEM((2, slots, tile_size, feat_width), panels.dtype),
            pltpu.SemaphoreType.DMA((2, slots)),
            pltpu.VMEM((2, tile_size, width), wide.dtype),
            pltpu.SemaphoreType.DMA((2,)),
        ],
        cost_estimate=pl.CostEstimate(flops=flops, bytes_accessed=moved, transcendentals=0),
    )(jnp.reshape(parity, (1,)).astype(jnp.int32), cols, wide, panels)


def shards(features, col_panels, block_counts, block_values, weight, bias, cotangent):
    sizes = {name: lax.axis_size(name) for name in ALL_AXES}
    rep_count = sizes["y_lo"] * sizes["core"]
    tile_size = block_values.shape[-1]
    feat_width = features.shape[1]
    own_panels = features.shape[0] // tile_size
    row_panels = col_panels.shape[0]
    global_cols = col_panels[:, 0, :]
    section_of = global_cols // (own_panels * rep_count)
    low = sizes["z"] * sizes["x"]
    gathered_pos = (section_of % low) * sizes["y_hi"] + section_of // low
    local_cols = gathered_pos * own_panels + global_cols % own_panels
    live_counts = block_counts[:, 0]
    tiles = block_values[:, 0]
    gathered = lax.all_gather(features, "y_hi", axis=0, tiled=True)
    gathered = lax.all_gather(gathered, ("z", "x"), axis=0, tiled=True)
    all_panels = gathered.reshape(-1, tile_size, feat_width)
    wide = _widen(live_counts, tiles)
    cols = jnp.clip(local_cols, 0, all_panels.shape[0] - 1).reshape(-1)
    cores = sizes["core"]
    me_core = lax.axis_index("core")
    sent = _aggregate(cols, wide, all_panels, cores - 1 - me_core, cores)
    arrived = lax.ppermute(sent, "core", _xor_perm(cores, 1))
    kept = _aggregate(cols, wide, all_panels, me_core, cores)
    half = kept + arrived
    summed_own = _halving_scatter(half, "y_lo", sizes["y_lo"], (0, 1))
    own_rows = own_panels * tile_size
    aggregated = summed_own.reshape(own_rows, feat_width).astype(jnp.bfloat16)
    pre = jnp.dot(aggregated, weight, preferred_element_type=jnp.float32) + bias
    hidden = jax.nn.silu(pre).astype(jnp.bfloat16)
    sigmoid_pre = jax.nn.sigmoid(pre)
    slope = (
        cotangent.astype(jnp.float32) * (sigmoid_pre * (1.0 + pre * (1.0 - sigmoid_pre)))
    ).astype(jnp.bfloat16)
    local_weight = jnp.einsum("nd,nf->df", aggregated, slope, preferred_element_type=jnp.float32)
    local_bias = jnp.sum(slope.astype(jnp.float32), axis=0)
    width = weight.shape[0]
    scatter_ways = sizes["core"] * sizes["x"]
    padded_rows = -(-(width + 1) // (scatter_ways * 8)) * scatter_ways * 8
    combined = jnp.zeros((padded_rows, feat_width), jnp.float32)
    combined = combined.at[:width].set(local_weight).at[width].set(local_bias)
    chunk = _halving_scatter(combined.reshape(sizes["core"], -1, feat_width), "core", sizes["core"], (0,))
    chunk = _halving_scatter(chunk.reshape(sizes["x"], -1, feat_width), "x", sizes["x"], (0, 1))
    for name in ("y_lo", "z", "y_hi"):
        chunk = _doubling_sum(chunk, name, sizes[name])
    chunk = _doubling_gather(chunk, "x", sizes["x"], (1, 0))
    chunk = _doubling_gather(chunk, "core", sizes["core"], (0,))
    node_total = lax.axis_size(SECTION_AXES) * rep_count * own_rows
    factor = 1.0 / math.sqrt(node_total)
    weight_sum = chunk[:width]
    bias_sum = chunk[width]
    return (hidden, weight_sum * factor, bias_sum * factor)


def solution(mesh):
    section_size, rep_size = mesh.devices.shape
    fine = Mesh(mesh.devices.reshape(2, section_size // 8, 4, rep_size // 2, 2), ALL_AXES)
    in_specs = (
        P(ALL_AXES, None),
        P(SECTION_AXES, REP_AXES, None),
        P(SECTION_AXES, REP_AXES),
        P(SECTION_AXES, REP_AXES, None, None, None),
        P(),
        P(),
        P(ALL_AXES, None),
    )
    out_specs = (P(ALL_AXES, None), P(), P())
    return jax.shard_map(shards, mesh=fine, in_specs=in_specs, out_specs=out_specs, check_vma=False)
```

```python
import math

import jax
import jax.numpy as jnp
from jax import lax
from jax.experimental import pallas as pl
from jax.experimental.pallas import tpu as pltpu
from jax.sharding import Mesh
from jax.sharding import PartitionSpec as P

SECTION_AXES = ("y_hi", "z", "x")
REP_AXES = ("y_lo", "core")
ALL_AXES = SECTION_AXES + REP_AXES


def _xor_perm(n, bit):
    return [(i, i ^ bit) for i in range(n)]


def _halving_scatter(blocks, axis, n, bits):
    me = lax.axis_index(axis)
    depth = n.bit_length() - 1
    rest = blocks.shape[1:]
    blocks = blocks.reshape((2,) * depth + rest)
    left = list(range(depth - 1, -1, -1))
    for bit in bits:
        at = left.index(bit)
        mine = (me // (1 << bit)) % 2
        keep = lax.dynamic_index_in_dim(blocks, mine, at, keepdims=False)
        send = lax.dynamic_index_in_dim(blocks, 1 - mine, at, keepdims=False)
        blocks = keep + lax.ppermute(send, axis, _xor_perm(n, 1 << bit))
        left.pop(at)
    return blocks


def _doubling_gather(piece, axis, n, bits):
    me = lax.axis_index(axis)
    rest = piece.shape
    got = []
    for bit in bits:
        other = lax.ppermute(piece, axis, _xor_perm(n, 1 << bit))
        upper = (me // (1 << bit)) % 2 == 1
        low = jnp.where(upper, other, piece)
        high = jnp.where(upper, piece, other)
        piece = jnp.stack([low, high])
        got = [bit] + got
    order = sorted(range(len(got)), key=lambda i: -got[i])
    piece = jnp.transpose(piece, order + list(range(len(got), piece.ndim)))
    return piece.reshape((n * rest[0],) + rest[1:])


def _doubling_sum(piece, axis, n):
    bit = 1
    while bit < n:
        piece = piece + lax.ppermute(piece, axis, _xor_perm(n, bit))
        bit *= 2
    return piece


def _aggregate_kernel(parity_ref, cols_ref, tiles_ref, panels_hbm, out_ref, buf, sems):
    groups, slots = out_ref.shape[0], buf.shape[1]
    stride = tiles_ref.shape[0] // groups
    parity = parity_ref[0]

    def copies(j, slot):
        g = stride * j + parity
        return [
            pltpu.make_async_copy(panels_hbm.at[cols_ref[g * slots + k]], buf.at[slot, k], sems.at[slot, k])
            for k in range(slots)
        ]

    pending = copies(0, 0)
    for c in pending:
        c.start()
    for j in range(groups):
        slot = j % 2
        if j + 1 < groups:
            ahead = copies(j + 1, 1 - slot)
            for c in ahead:
                c.start()
        for c in pending:
            c.wait()
        rhs = buf[slot].reshape(slots * buf.shape[2], buf.shape[3])
        out_ref[j] = jnp.dot(tiles_ref[stride * j + parity], rhs, preferred_element_type=jnp.float32)
        if j + 1 < groups:
            pending = ahead


def _widen(counts, tiles):
    groups, slots, tile_size, _ = tiles.shape
    live = jnp.arange(slots, dtype=jnp.int32)[None, :] < counts[:, None]
    wide = jnp.where(live[:, :, None, None], tiles, jnp.zeros((), tiles.dtype))
    return wide.transpose(0, 2, 1, 3).reshape(groups, tile_size, slots * tile_size)


def _aggregate(cols, wide, panels, parity, stride):
    groups, tile_size, width = wide.shape
    slots = width // tile_size
    feat_width = panels.shape[-1]
    picked = groups // stride
    flops = 2 * picked * slots * tile_size * tile_size * feat_width
    moved = (picked * tile_size * width * 2 + picked * slots * tile_size * feat_width * 2
             + picked * tile_size * feat_width * 4)
    return pl.pallas_call(
        _aggregate_kernel,
        out_shape=jax.ShapeDtypeStruct((picked, tile_size, feat_width), jnp.float32),
        in_specs=[
            pl.BlockSpec(memory_space=pltpu.SMEM),
            pl.BlockSpec(memory_space=pltpu.SMEM),
            pl.BlockSpec(memory_space=pltpu.VMEM),
            pl.BlockSpec(memory_space=pl.ANY),
        ],
        out_specs=pl.BlockSpec(memory_space=pltpu.VMEM),
        scratch_shapes=[
            pltpu.VMEM((2, slots, tile_size, feat_width), panels.dtype),
            pltpu.SemaphoreType.DMA((2, slots)),
        ],
        cost_estimate=pl.CostEstimate(flops=flops, bytes_accessed=moved, transcendentals=0),
    )(jnp.reshape(parity, (1,)).astype(jnp.int32), cols, wide, panels)


def shards(features, col_panels, block_counts, block_values, weight, bias, cotangent):
    sizes = {name: lax.axis_size(name) for name in ALL_AXES}
    rep_count = sizes["y_lo"] * sizes["core"]
    tile_size = block_values.shape[-1]
    feat_width = features.shape[1]
    own_panels = features.shape[0] // tile_size
    row_panels = col_panels.shape[0]
    global_cols = col_panels[:, 0, :]
    section_of = global_cols // (own_panels * rep_count)
    low = sizes["z"] * sizes["x"]
    gathered_pos = (section_of % low) * sizes["y_hi"] + section_of // low
    local_cols = gathered_pos * own_panels + global_cols % own_panels
    live_counts = block_counts[:, 0]
    tiles = block_values[:, 0]
    gathered = lax.all_gather(features, "y_hi", axis=0, tiled=True)
    gathered = lax.all_gather(gathered, ("z", "x"), axis=0, tiled=True)
    all_panels = gathered.reshape(-1, tile_size, feat_width)
    wide = _widen(live_counts, tiles)
    cols = jnp.clip(local_cols, 0, all_panels.shape[0] - 1).reshape(-1)
    cores = sizes["core"]
    me_core = lax.axis_index("core")
    sent = _aggregate(cols, wide, all_panels, cores - 1 - me_core, cores)
    arrived = lax.ppermute(sent, "core", _xor_perm(cores, 1))
    kept = _aggregate(cols, wide, all_panels, me_core, cores)
    half = kept + arrived
    summed_own = _halving_scatter(half, "y_lo", sizes["y_lo"], (0, 1))
    own_rows = own_panels * tile_size
    aggregated = summed_own.reshape(own_rows, feat_width).astype(jnp.bfloat16)
    pre = jnp.dot(aggregated, weight, preferred_element_type=jnp.float32) + bias
    hidden = jax.nn.silu(pre).astype(jnp.bfloat16)
    sigmoid_pre = jax.nn.sigmoid(pre)
    slope = (
        cotangent.astype(jnp.float32) * (sigmoid_pre * (1.0 + pre * (1.0 - sigmoid_pre)))
    ).astype(jnp.bfloat16)
    local_weight = jnp.einsum("nd,nf->df", aggregated, slope, preferred_element_type=jnp.float32)
    local_bias = jnp.sum(slope.astype(jnp.float32), axis=0)
    width = weight.shape[0]
    scatter_ways = sizes["core"] * sizes["x"]
    padded_rows = -(-(width + 1) // scatter_ways) * scatter_ways
    combined = jnp.zeros((padded_rows, feat_width), jnp.float32)
    combined = combined.at[:width].set(local_weight).at[width].set(local_bias)
    chunk = _halving_scatter(combined.reshape(sizes["core"], -1, feat_width), "core", sizes["core"], (0,))
    chunk = _halving_scatter(chunk.reshape(sizes["x"], -1, feat_width), "x", sizes["x"], (0, 1))
    for name in ("y_lo", "z", "y_hi"):
        chunk = _doubling_sum(chunk, name, sizes[name])
    chunk = _doubling_gather(chunk, "x", sizes["x"], (1, 0))
    chunk = _doubling_gather(chunk, "core", sizes["core"], (0,))
    node_total = lax.axis_size(SECTION_AXES) * rep_count * own_rows
    factor = 1.0 / math.sqrt(node_total)
    weight_sum = chunk[:width]
    bias_sum = chunk[width]
    return (hidden, weight_sum * factor, bias_sum * factor)


def solution(mesh):
    section_size, rep_size = mesh.devices.shape
    fine = Mesh(mesh.devices.reshape(2, section_size // 8, 4, rep_size // 2, 2), ALL_AXES)
    in_specs = (
        P(ALL_AXES, None),
        P(SECTION_AXES, REP_AXES, None),
        P(SECTION_AXES, REP_AXES),
        P(SECTION_AXES, REP_AXES, None, None, None),
        P(),
        P(),
        P(ALL_AXES, None),
    )
    out_specs = (P(ALL_AXES, None), P(), P())
    return jax.shard_map(shards, mesh=fine, in_specs=in_specs, out_specs=out_specs, check_vma=False)
```
